32 devices in a mesh: dp: 16 (over z, y, core), tensor: 2 (over x).
Axes of the slice: x: 2, y: 2, z: 4, core: 2. Of those that a mesh axis runs over, the one named last changes fastest.
Arguments:
- hidden_states: bfloat16 [8192, 2048], P('dp', 'tensor'), may hold values from -6 to 6
- norm_gain: bfloat16 [2048], replicated, may hold values from 0.25 to 1.75
- head_weight: bfloat16 [2048, 25600], P(None, ('tensor', 'dp')), may hold values from -1 to 1
- target_ids: int32 [8192], P('dp'), may hold values from 0 to 25599
- loss_mask: int32 [8192], P('dp'), may hold values from 0 to 1, as said below
- seq_lengths: int32 [16], replicated, may hold values from 1 to 4096, as said below
- slot_order: int32 [16], replicated, may hold values from 0 to 15, each once
Outputs:
- token_logprob: float32 [8192], P(('dp', 'tensor'))
- token_entropy: float32 [8192], P(('dp', 'tensor'))
- seq_mean_logprob: float32 [16], P('dp')
- seq_mean_entropy: float32 [16], P('dp')
The draws below stay inside these ranges and needn't reach their ends.
Inputs may be any that keep to these rules, and one draw needn't show every extreme that they name: `seq_lengths`: sequences lie in packed order, one after another; their lengths sum to 8192; the longest has exactly 4096 tokens and some sequence has exactly 1 token. `slot_order`: each sequence appears once. `loss_mask`: some sequence of exactly 1 token has no scored row.
All inputs are finite; a program needn't handle non-finite values.
Results may differ from the reference program's by a relative error of at most 0.0012.
Values may be sent and summed in bfloat16 or wider, within the bound.
No kernel may reach another device: no remote copies, remote signals or barrier semaphores. Data moves between devices by JAX's collectives and lax.ppermute only.
A program may use at most 192 MiB of HBM per device.

```python
import math
import jax
import jax.numpy as jnp
import numpy as np
from jax import lax

D = 2048
VOCAB = 25600
LEN = 4096
TOKENS = 8192
SEQS = 16


def direction_pair(key):
    first = jnp.clip(jax.random.normal(jax.random.fold_in(key, 21), (D,), jnp.float32), -4.0, 4.0)
    second = jnp.clip(jax.random.normal(jax.random.fold_in(key, 22), (D,), jnp.float32), -4.0, 4.0)
    return (first, second)


def draw_hidden_states(key, part):
    base = jnp.clip(jax.random.normal(jax.random.fold_in(key, 11), (TOKENS, D), jnp.float32), -6.0, 6.0)
    first, second = direction_pair(key)
    rows = jnp.arange(TOKENS)[:, None] % 61
    base = jnp.where(rows == 7, first[None, :], base)
    base = jnp.where(rows == 30, second[None, :], base)
    return base.astype(jnp.bfloat16)


def draw_head_weight(key, part):
    scale = 3.0 / math.sqrt(D)
    base = jnp.clip(jax.random.normal(jax.random.fold_in(key, 12), (D, VOCAB), jnp.float32), -5.0, 5.0) * scale
    cols = jnp.arange(VOCAB)[None, :]
    half = VOCAB // 2
    first, second = direction_pair(key)
    strong = 225.0 / D
    middle = 145.0 / D
    base = jnp.where(cols == 3, strong * first[:, None], base)
    base = jnp.where(cols == 4, strong * 1.009 * first[:, None], base)
    base = jnp.where(cols == half + 1, middle * second[:, None], base)
    base = jnp.where(cols == half + 2, middle * 1.015 * second[:, None], base)
    limit = max(0.75, 960.0 / D)
    base = jnp.clip(base, -limit, limit)
    row_ids = jnp.arange(D)[:, None]
    plus_row = jax.random.randint(jax.random.fold_in(key, 51), (), 0, D)
    minus_row = (plus_row + 1) % D
    plus_column = jax.random.randint(jax.random.fold_in(key, 52), (), 8, half)
    minus_column = jax.random.randint(jax.random.fold_in(key, 53), (), half + 8, VOCAB)
    base = jnp.where((row_ids == plus_row) & (cols == plus_column), 1.0, base)
    base = jnp.where((row_ids == minus_row) & (cols == minus_column), -1.0, base)
    return base.astype(jnp.bfloat16)


def packed_lengths(key):
    others = SEQS - 2
    leftover = TOKENS - LEN - 1 - others
    even_share = leftover // others
    surplus = leftover - even_share * others
    spread_limit = max(0, min(even_share, LEN - 2 - even_share))
    raw_draws = jax.random.randint(jax.random.fold_in(key, 41), (others,), 0, spread_limit + 1).astype(jnp.int32)
    lifted = raw_draws * raw_draws // max(spread_limit, 1)
    shifted = lifted - jnp.roll(lifted, 1)
    rank_order = jax.random.permutation(jax.random.fold_in(key, 42), others).astype(jnp.int32)
    topped = (rank_order < surplus).astype(jnp.int32)
    other_lengths = 1 + even_share + shifted + topped
    length_table = jnp.concatenate([jnp.array([LEN, 1], jnp.int32), other_lengths.astype(jnp.int32)])
    placing = jax.random.permutation(jax.random.fold_in(key, 43), SEQS).astype(jnp.int32)
    lengths = length_table[placing]
    short_index = jnp.sum(jnp.where(placing == 1, jnp.arange(SEQS, dtype=jnp.int32), 0))
    return (lengths.astype(jnp.int32), short_index)


def draw_seq_lengths(key, part):
    lengths, short_index = packed_lengths(key)
    return lengths


def draw_loss_mask(key, part):
    lengths, short_index = packed_lengths(key)
    ends = jnp.cumsum(lengths)
    short_row = jnp.sum(jnp.where(jnp.arange(SEQS, dtype=jnp.int32) == short_index, ends, 0)) - 1
    coin_draws = jax.random.randint(jax.random.fold_in(key, 44), (TOKENS,), 0, 4)
    row_ids = jnp.arange(TOKENS, dtype=jnp.int32)
    return jnp.where((coin_draws < 3) & (row_ids != short_row), 1, 0).astype(jnp.int32)


def touch_ends(result, rng, least, high):
    shape = result.shape
    place = [jax.random.randint(jax.random.fold_in(rng, axis), (), 0, shape[axis]) for axis in range(len(shape))]
    result = result.at[tuple(place)].set(least)
    longest = shape.index(max(shape))
    place[longest] = (place[longest] + 1) % shape[longest]
    return result.at[tuple(place)].set(high)


def rank_bounds(amount, lean):
    weights = [(1 << 20) // math.isqrt(grade ** lean) + 1 for grade in range(1, amount + 1)]
    scale = 1 + sum(weights) // (1 << 30)
    return np.cumsum(np.array([max(1, weight // scale) for weight in weights]))


def skewed_ids(own_key, dims, number_of, lean):
    grid = rank_bounds(number_of, lean)
    pick = jax.random.randint(jax.random.fold_in(own_key, 1), dims, 0, int(grid[number_of - 1]))
    standing = jnp.searchsorted(jnp.asarray(grid, jnp.int32), pick, side="right")
    return jax.random.permutation(jax.random.fold_in(own_key, 2), number_of)[standing].astype(jnp.int32)


def setup_inputs(seed: int = 0) -> dict:
    key_of = jax.random.split(jax.random.key(seed), 8)
    hidden_states = draw_hidden_states(jax.random.fold_in(key_of[7], 71), 0)
    norm_gain = jnp.clip(1.0 + 0.15 * jax.random.normal(key_of[1], (D,), jnp.float32), 0.25, 1.75).astype(jnp.bfloat16)
    head_weight = draw_head_weight(jax.random.fold_in(key_of[7], 71), 0)
    target_ids = touch_ends(skewed_ids(key_of[3], (TOKENS,), VOCAB, 2), jax.random.fold_in(key_of[3], 3), 0, VOCAB - 1).astype(jnp.int32)
    loss_mask = draw_loss_mask(jax.random.fold_in(key_of[7], 71), 0)
    seq_lengths = draw_seq_lengths(jax.random.fold_in(key_of[7], 71), 0)
    slot_order = jax.random.permutation(key_of[6], SEQS).astype(jnp.int32)
    return {"hidden_states": hidden_states, "norm_gain": norm_gain, "head_weight": head_weight, "target_ids": target_ids, "loss_mask": loss_mask, "seq_lengths": seq_lengths, "slot_order": slot_order}


EPS = 1e-05

def normalize(hidden_states, norm_gain):
    values = hidden_states.astype(jnp.float32)
    square = lax.optimization_barrier(jnp.mean(values * values, axis=1, keepdims=True))
    return (values * lax.rsqrt(square + EPS) * norm_gain.astype(jnp.float32)).astype(jnp.bfloat16)

def reference(hidden_states, norm_gain, head_weight, target_ids, loss_mask, seq_lengths, slot_order):
    normed = normalize(hidden_states, norm_gain)
    block = math.gcd(TOKENS, 512)

    def one_block(pair):
        rows, wanted = pair
        logits = jnp.dot(rows, head_weight, preferred_element_type=jnp.float32)
        top = lax.optimization_barrier(jnp.max(logits, axis=1))
        shifted = logits - top[:, None]
        expo = jnp.exp(shifted)
        total = lax.optimization_barrier(jnp.sum(expo, axis=1))
        spread = lax.optimization_barrier(jnp.sum(expo * shifted, axis=1))
        picked = jnp.take_along_axis(logits, wanted[:, None].astype(jnp.int32), axis=1)[:, 0]
        logsum = jnp.log(total)
        return (picked - top - logsum, logsum - spread / total)
    log_prob, entropy = lax.map(one_block, (normed.reshape(-1, block, D), target_ids.reshape(-1, block)))
    live = loss_mask.astype(jnp.float32)
    token_logprob = log_prob.reshape(-1) * live
    token_entropy = entropy.reshape(-1) * live
    ends = jnp.cumsum(seq_lengths).astype(jnp.int32)
    row_index = jnp.arange(TOKENS, dtype=jnp.int32)
    segment = lax.optimization_barrier(jnp.sum((row_index[:, None] >= ends[None, :]).astype(jnp.int32), axis=1)).astype(jnp.int32)
    lp_sum = jax.ops.segment_sum(token_logprob, segment, num_segments=SEQS)
    ent_sum = jax.ops.segment_sum(token_entropy, segment, num_segments=SEQS)
    count = jax.ops.segment_sum(live, segment, num_segments=SEQS)
    floor = jnp.maximum(count[slot_order], 1.0)
    return (token_logprob, token_entropy, lp_sum[slot_order] / floor, ent_sum[slot_order] / floor)
```

```python
import jax
import jax.numpy as jnp
import numpy as np
from jax import lax
from jax.sharding import Mesh
from jax.sharding import PartitionSpec as P

EPS = 1e-05
ROWS = ("dh", "p", "dl")
ALL = ("dh", "p", "dl", "t")


def swap(x, name):
    return lax.ppermute(x, name, [(0, 1), (1, 0)])


def whole_rows(x, t, nt):
    if nt == 2:
        other = swap(x, "t")
        return jnp.where(t == 0, jnp.concatenate([x, other], 1), jnp.concatenate([other, x], 1))
    return lax.all_gather(x, "t", axis=1, tiled=True)


def shifted(x, s, n, dh):
    if s == 0:
        return x
    if n <= 4:
        return lax.ppermute(x, "dh", [(i, (i + s) % n) for i in range(n)])
    return None


def per_device(hidden_states, norm_gain, head_weight, target_ids, loss_mask, seq_lengths, slot_order):
    rb, dt = hidden_states.shape
    nt = lax.axis_size("t")
    n = lax.axis_size("dh")
    nd = n * 4
    d = dt * nt
    cb = head_weight.shape[1]
    t = lax.axis_index("t")
    dh = lax.axis_index("dh")
    p = lax.axis_index("p")
    dl = lax.axis_index("dl")
    b = (dh * 2 + p) * 2 + dl

    w_p = swap(head_weight, "p")
    w_pair = jnp.concatenate([head_weight, w_p], 1)
    w_all = jnp.concatenate([w_pair, swap(w_pair, "dl")], 1)
    block_of = jnp.stack([b, (dh * 2 + 1 - p) * 2 + dl, (dh * 2 + p) * 2 + 1 - dl, (dh * 2 + 1 - p) * 2 + 1 - dl])
    column = ((t * nd + block_of)[:, None] * cb + jnp.arange(cb, dtype=jnp.int32)[None, :]).reshape(-1)

    gain = norm_gain.astype(jnp.float32)
    if n > 4:
        gathered_h = lax.all_gather(hidden_states, "dh", axis=0, tiled=False)
        gathered_t = lax.all_gather(target_ids, "dh", axis=0, tiled=False)

    stats = []
    for s in range(n):
        if n > 4:
            src = (dh - s) % n
            h_s, t_s = gathered_h[src], gathered_t[src]
        else:
            h_s, t_s = shifted(hidden_states, s, n, dh), shifted(target_ids, s, n, dh)
        values = whole_rows(h_s, t, nt).astype(jnp.float32)
        square = jnp.mean(values * values, axis=1, keepdims=True)
        normed = (values * lax.rsqrt(square + EPS) * gain[None, :]).astype(jnp.bfloat16)
        logits = jnp.dot(normed, w_all, preferred_element_type=jnp.float32)
        top = jnp.max(logits, axis=1)
        shift = logits - top[:, None]
        expo = jnp.exp(shift)
        total = jnp.sum(expo, axis=1)
        spread = jnp.sum(expo * shift, axis=1)
        picked = jnp.sum(jnp.where(column[None, :] == t_s[:, None], logits, 0.0), axis=1)
        stats.append(jnp.stack([top, total, spread, picked]))
    stats = jnp.stack(stats)
    stats = jnp.take(stats, (dh - jnp.arange(n)) % n, axis=0)
    rq = rb // nt
    stats = stats.reshape(n, 4, nt, rq).transpose(0, 2, 1, 3).reshape(n * nt, 4, rq)
    got = lax.all_to_all(stats, ("dh", "t"), 0, 0, tiled=True)
    tops, totals, spreads, pickeds = got[:, 0], got[:, 1], got[:, 2], got[:, 3]
    row_top = jnp.max(tops, axis=0)
    scale = jnp.exp(tops - row_top[None, :])
    row_total = jnp.sum(totals * scale, axis=0)
    row_spread = jnp.sum(scale * (spreads + totals * (tops - row_top[None, :])), axis=0)
    row_picked = jnp.sum(pickeds, axis=0)

    logsum = jnp.log(row_total)
    live = lax.dynamic_slice_in_dim(loss_mask, t * rq, rq).astype(jnp.float32)
    token_logprob = (row_picked - row_top - logsum) * live
    token_entropy = (logsum - row_spread / row_total) * live

    seqs = slot_order.shape[0]
    ends = jnp.cumsum(seq_lengths)
    position = b * rb + t * rq + jnp.arange(rq, dtype=jnp.int32)
    segment = jnp.sum((position[:, None] >= ends[None, :]).astype(jnp.int32), axis=1)
    member = (segment[:, None] == slot_order[None, :]).astype(jnp.float32)
    lp_part = jnp.dot(token_logprob, member, precision=lax.Precision.HIGHEST)
    ent_part = jnp.dot(token_entropy, member, precision=lax.Precision.HIGHEST)
    count_part = jnp.dot(live, member, precision=lax.Precision.HIGHEST)
    k = seqs // nd
    parts = jnp.stack([lp_part, ent_part, count_part]).reshape(3, nd, k).transpose(1, 0, 2)
    parts = jnp.broadcast_to(parts[:, None], (nd, nt, 3, k)).reshape(nd * nt, 3, k)
    sums = jnp.sum(lax.all_to_all(parts, ALL, 0, 0, tiled=True), axis=0)
    floor = jnp.maximum(sums[2], 1.0)
    return (token_logprob, token_entropy, sums[0] / floor, sums[1] / floor)


def solution(mesh):
    nd, nt = mesh.devices.shape
    grid = Mesh(mesh.devices.reshape(nd // 4, 2, 2, nt), ALL)
    placed = (P(ROWS, "t"), P(), P(None, ("t",) + ROWS), P(ROWS), P(ROWS), P(), P())
    return jax.shard_map(
        per_device,
        mesh=grid,
        in_specs=placed,
        out_specs=(P(ALL), P(ALL), P(ROWS), P(ROWS)),
        check_vma=False,
    )
```

```python
import jax
import jax.numpy as jnp
import numpy as np
from jax import lax
from jax.sharding import Mesh
from jax.sharding import PartitionSpec as P

EPS = 1e-05
ROWS = ("dh", "p", "dl")
ALL = ("dh", "p", "dl", "t")


def swap(x, name):
    return lax.ppermute(x, name, [(0, 1), (1, 0)])


def whole_rows(x, t, nt, other=None):
    if nt == 2:
        if other is None:
            other = swap(x, "t")
        return jnp.where(t == 0, jnp.concatenate([x, other], 1), jnp.concatenate([other, x], 1))
    return lax.all_gather(x, "t", axis=1, tiled=True)


def shifted(x, s, n, dh):
    if s == 0:
        return x
    if n <= 4:
        return lax.ppermute(x, "dh", [(i, (i + s) % n) for i in range(n)])
    return None


def per_device(hidden_states, norm_gain, head_weight, target_ids, loss_mask, seq_lengths, slot_order):
    rb, dt = hidden_states.shape
    nt = lax.axis_size("t")
    n = lax.axis_size("dh")
    nd = n * 4
    d = dt * nt
    cb = head_weight.shape[1]
    t = lax.axis_index("t")
    dh = lax.axis_index("dh")
    p = lax.axis_index("p")
    dl = lax.axis_index("dl")
    b = (dh * 2 + p) * 2 + dl

    w_p = swap(head_weight, "p")
    block_of = jnp.stack([b, (dh * 2 + 1 - p) * 2 + dl, (dh * 2 + p) * 2 + 1 - dl, (dh * 2 + 1 - p) * 2 + 1 - dl])
    column = ((t * nd + block_of)[:, None] * cb + jnp.arange(cb, dtype=jnp.int32)[None, :]).reshape(-1)

    gain = norm_gain.astype(jnp.float32)
    if n > 4:
        gathered_h = lax.all_gather(hidden_states, "dh", axis=0, tiled=False)
        gathered_t = lax.all_gather(target_ids, "dh", axis=0, tiled=False)

    else:
        extra = (2 * rb) // dt if (2 * rb) % dt == 0 else 0
        if extra:
            code = jnp.concatenate([target_ids // 128, target_ids % 128]).astype(jnp.bfloat16).reshape(extra, dt)
            carried = jnp.concatenate([hidden_states, code], 0)
            moved = [shifted(carried, s, n, dh) for s in range(1, n)]
            moved_t = []
        else:
            moved = [shifted(hidden_states, s, n, dh) for s in range(1, n)]
            moved_t = [shifted(target_ids, s, n, dh) for s in range(1, n)]
        own_other = swap(hidden_states, "t") if nt == 2 else hidden_states
        w_p, own_other, moved, moved_t = lax.optimization_barrier((w_p, own_other, moved, moved_t))
        if extra:
            moved_t = []
            for block in moved:
                parts = block[rb:].reshape(2, rb).astype(jnp.int32)
                moved_t.append(parts[0] * 128 + parts[1])
            moved = [block[:rb] for block in moved]

    w_pair = jnp.concatenate([head_weight, w_p], 1)
    w_all = jnp.concatenate([w_pair, swap(w_pair, "dl")], 1)

    stats = []
    for s in range(n):
        if n > 4:
            src = (dh - s) % n
            h_s, t_s = gathered_h[src], gathered_t[src]
            values = whole_rows(h_s, t, nt)
        elif s == 0:
            h_s, t_s = hidden_states, target_ids
            values = whole_rows(h_s, t, nt, own_other if nt == 2 else None)
        else:
            h_s, t_s = moved[s - 1], moved_t[s - 1]
            values = whole_rows(h_s, t, nt)
        values = values.astype(jnp.float32)
        square = jnp.mean(values * values, axis=1, keepdims=True)
        normed = (values * lax.rsqrt(square + EPS) * gain[None, :]).astype(jnp.bfloat16)
        logits = jnp.dot(normed, w_all, preferred_element_type=jnp.float32)
        top = jnp.max(logits, axis=1)
        shift = logits - top[:, None]
        expo = jnp.exp(shift)
        total = jnp.sum(expo, axis=1)
        spread = jnp.sum(expo * shift, axis=1)
        picked = jnp.sum(jnp.where(column[None, :] == t_s[:, None], logits, 0.0), axis=1)
        stats.append(jnp.stack([top, total, spread, picked]))
    stats = jnp.stack(stats)
    stats = jnp.take(stats, (dh - jnp.arange(n)) % n, axis=0)
    rq = rb // nt
    stats = stats.reshape(n, 4, nt, rq).transpose(0, 2, 1, 3).reshape(n * nt, 4, rq)
    got = lax.all_to_all(stats, ("dh", "t"), 0, 0, tiled=True)
    tops, totals, spreads, pickeds = got[:, 0], got[:, 1], got[:, 2], got[:, 3]
    row_top = jnp.max(tops, axis=0)
    scale = jnp.exp(tops - row_top[None, :])
    row_total = jnp.sum(totals * scale, axis=0)
    row_spread = jnp.sum(scale * (spreads + totals * (tops - row_top[None, :])), axis=0)
    row_picked = jnp.sum(pickeds, axis=0)

    logsum = jnp.log(row_total)
    live = lax.dynamic_slice_in_dim(loss_mask, t * rq, rq).astype(jnp.float32)
    token_logprob = (row_picked - row_top - logsum) * live
    token_entropy = (logsum - row_spread / row_total) * live

    seqs = slot_order.shape[0]
    ends = jnp.cumsum(seq_lengths)
    position = b * rb + t * rq + jnp.arange(rq, dtype=jnp.int32)
    segment = jnp.sum((position[:, None] >= ends[None, :]).astype(jnp.int32), axis=1)
    member = (segment[:, None] == slot_order[None, :]).astype(jnp.float32)
    lp_part = jnp.dot(token_logprob, member, precision=lax.Precision.HIGHEST)
    ent_part = jnp.dot(token_entropy, member, precision=lax.Precision.HIGHEST)
    count_part = jnp.dot(live, member, precision=lax.Precision.HIGHEST)
    k = seqs // nd
    parts = jnp.stack([lp_part, ent_part, count_part]).reshape(3, nd, k).transpose(1, 0, 2)
    parts = jnp.broadcast_to(parts[:, None], (nd, nt, 3, k)).reshape(nd * nt, 3, k)
    sums = jnp.sum(lax.all_to_all(parts, ALL, 0, 0, tiled=True), axis=0)
    floor = jnp.maximum(sums[2], 1.0)
    return (token_logprob, token_entropy, sums[0] / floor, sums[1] / floor)


def solution(mesh):
    nd, nt = mesh.devices.shape
    grid = Mesh(mesh.devices.reshape(nd // 4, 2, 2, nt), ALL)
    placed = (P(ROWS, "t"), P(), P(None, ("t",) + ROWS), P(ROWS), P(ROWS), P(), P())
    return jax.shard_map(
        per_device,
        mesh=grid,
        in_specs=placed,
        out_specs=(P(ALL), P(ALL), P(ROWS), P(ROWS)),
        check_vma=False,
    )
```

```python
import jax
import jax.numpy as jnp
import numpy as np
from jax import lax
from jax.sharding import Mesh
from jax.sharding import PartitionSpec as P

EPS = 1e-05
ROWS = ("dh", "p", "dl")
ALL = ("dh", "p", "dl", "t")


def swap(x, name):
    return lax.ppermute(x, name, [(0, 1), (1, 0)])


def whole_rows(x, t, nt, other=None):
    if nt == 2:
        if other is None:
            other = swap(x, "t")
        return jnp.where(t == 0, jnp.concatenate([x, other], 1), jnp.concatenate([other, x], 1))
    return lax.all_gather(x, "t", axis=1, tiled=True)


def shifted(x, s, n, dh):
    if s == 0:
        return x
    if n <= 4:
        return lax.ppermute(x, "dh", [(i, (i + s) % n) for i in range(n)])
    return None


def per_device(hidden_states, norm_gain, head_weight, target_ids, loss_mask, seq_lengths, slot_order):
    rb, dt = hidden_states.shape
    nt = lax.axis_size("t")
    n = lax.axis_size("dh")
    nd = n * 4
    d = dt * nt
    cb = head_weight.shape[1]
    t = lax.axis_index("t")
    dh = lax.axis_index("dh")
    p = lax.axis_index("p")
    dl = lax.axis_index("dl")
    b = (dh * 2 + p) * 2 + dl

    w_p = swap(head_weight, "p")
    block_of = jnp.stack([b, (dh * 2 + 1 - p) * 2 + dl, (dh * 2 + p) * 2 + 1 - dl, (dh * 2 + 1 - p) * 2 + 1 - dl])
    column = ((t * nd + block_of)[:, None] * cb + jnp.arange(cb, dtype=jnp.int32)[None, :]).reshape(-1)

    gain = norm_gain.astype(jnp.float32)
    if n > 4:
        gathered_h = lax.all_gather(hidden_states, "dh", axis=0, tiled=False)
        gathered_t = lax.all_gather(target_ids, "dh", axis=0, tiled=False)

    else:
        extra = (2 * rb) // dt if (2 * rb) % dt == 0 else 0
        if extra:
            code = jnp.concatenate([target_ids // 128, target_ids % 128]).astype(jnp.bfloat16).reshape(extra, dt)
            carried = jnp.concatenate([hidden_states, code], 0)
            moved = [shifted(carried, s, n, dh) for s in range(1, n)]
            moved_t = []
        else:
            moved = [shifted(hidden_states, s, n, dh) for s in range(1, n)]
            moved_t = [shifted(target_ids, s, n, dh) for s in range(1, n)]
        own_other = swap(hidden_states, "t") if nt == 2 else hidden_states
        w_p, own_other, moved, moved_t = lax.optimization_barrier((w_p, own_other, moved, moved_t))
        if extra:
            moved_t = []
            for block in moved:
                parts = block[rb:].reshape(2, rb).astype(jnp.int32)
                moved_t.append(parts[0] * 128 + parts[1])
            moved = [block[:rb] for block in moved]

    w_pair = jnp.concatenate([head_weight, w_p], 1)

    def block_stats(values, t_s, w_all):
        values = values.astype(jnp.float32)
        square = jnp.mean(values * values, axis=1, keepdims=True)
        normed = (values * lax.rsqrt(square + EPS) * gain[None, :]).astype(jnp.bfloat16)
        logits = jnp.dot(normed, w_all, preferred_element_type=jnp.float32)
        top = jnp.max(logits, axis=1)
        shift = logits - top[:, None]
        expo = jnp.exp(shift)
        total = jnp.sum(expo, axis=1)
        spread = jnp.sum(expo * shift, axis=1)
        picked = jnp.sum(jnp.where(column[None, :] == t_s[:, None], logits, 0.0), axis=1)
        return jnp.stack([top, total, spread, picked])

    def joined(x, other):
        return jnp.where(t == 0, jnp.concatenate([x, other], 1), jnp.concatenate([other, x], 1))

    stats = []
    if n <= 4 and nt == 2:
        w_dl = swap(w_pair, "dl")
        other = {}
        if n > 1:
            w_dl, other[1] = lax.optimization_barrier((w_dl, swap(moved[0], "t")))
        w_all = jnp.concatenate([w_pair, w_dl], 1)
        for s in range(n):
            if s == 0:
                values = joined(hidden_states, own_other)
                t_s = target_ids
            else:
                values = joined(moved[s - 1], other[s])
                t_s = moved_t[s - 1]
            block = block_stats(values, t_s, w_all)
            if s + 2 < n:
                block, other[s + 2] = lax.optimization_barrier((block, swap(moved[s + 1], "t")))
            stats.append(block)
    else:
        w_all = jnp.concatenate([w_pair, swap(w_pair, "dl")], 1)
        for s in range(n):
            if n > 4:
                src = (dh - s) % n
                h_s, t_s = gathered_h[src], gathered_t[src]
                values = whole_rows(h_s, t, nt)
            elif s == 0:
                h_s, t_s = hidden_states, target_ids
                values = whole_rows(h_s, t, nt)
            else:
                h_s, t_s = moved[s - 1], moved_t[s - 1]
                values = whole_rows(h_s, t, nt)
            stats.append(block_stats(values, t_s, w_all))
    stats = jnp.stack(stats)
    stats = jnp.take(stats, (dh - jnp.arange(n)) % n, axis=0)
    rq = rb // nt
    stats = stats.reshape(n, 4, nt, rq).transpose(0, 2, 1, 3).reshape(n * nt, 4, rq)
    got = lax.all_to_all(stats, ("dh", "t"), 0, 0, tiled=True)
    tops, totals, spreads, pickeds = got[:, 0], got[:, 1], got[:, 2], got[:, 3]
    row_top = jnp.max(tops, axis=0)
    scale = jnp.exp(tops - row_top[None, :])
    row_total = jnp.sum(totals * scale, axis=0)
    row_spread = jnp.sum(scale * (spreads + totals * (tops - row_top[None, :])), axis=0)
    row_picked = jnp.sum(pickeds, axis=0)

    logsum = jnp.log(row_total)
    live = lax.dynamic_slice_in_dim(loss_mask, t * rq, rq).astype(jnp.float32)
    token_logprob = (row_picked - row_top - logsum) * live
    token_entropy = (logsum - row_spread / row_total) * live

    seqs = slot_order.shape[0]
    ends = jnp.cumsum(seq_lengths)
    position = b * rb + t * rq + jnp.arange(rq, dtype=jnp.int32)
    segment = jnp.sum((position[:, None] >= ends[None, :]).astype(jnp.int32), axis=1)
    member = (segment[:, None] == slot_order[None, :]).astype(jnp.float32)
    lp_part = jnp.dot(token_logprob, member, precision=lax.Precision.HIGHEST)
    ent_part = jnp.dot(token_entropy, member, precision=lax.Precision.HIGHEST)
    count_part = jnp.dot(live, member, precision=lax.Precision.HIGHEST)
    k = seqs // nd
    parts = jnp.stack([lp_part, ent_part, count_part]).reshape(3, nd, k).transpose(1, 0, 2)
    parts = jnp.broadcast_to(parts[:, None], (nd, nt, 3, k)).reshape(nd * nt, 3, k)
    sums = jnp.sum(lax.all_to_all(parts, ALL, 0, 0, tiled=True), axis=0)
    floor = jnp.maximum(sums[2], 1.0)
    return (token_logprob, token_entropy, sums[0] / floor, sums[1] / floor)


def solution(mesh):
    nd, nt = mesh.devices.shape
    grid = Mesh(mesh.devices.reshape(nd // 4, 2, 2, nt), ALL)
    placed = (P(ROWS, "t"), P(), P(None, ("t",) + ROWS), P(ROWS), P(ROWS), P(), P())
    return jax.shard_map(
        per_device,
        mesh=grid,
        in_specs=placed,
        out_specs=(P(ALL), P(ALL), P(ROWS), P(ROWS)),
        check_vma=False,
    )
```

```python
import jax
import jax.numpy as jnp
import numpy as np
from jax import lax
from jax.sharding import Mesh
from jax.sharding import PartitionSpec as P

EPS = 1e-05
ROWS = ("dh", "p", "dl")
ALL = ("dh", "p", "dl", "t")


def swap(x, name):
    return lax.ppermute(x, name, [(0, 1), (1, 0)])


def whole_rows(x, t, nt, other=None):
    if nt == 2:
        if other is None:
            other = swap(x, "t")
        return jnp.where(t == 0, jnp.concatenate([x, other], 1), jnp.concatenate([other, x], 1))
    return lax.all_gather(x, "t", axis=1, tiled=True)


def shifted(x, s, n, dh):
    if s == 0:
        return x
    if n <= 4:
        return lax.ppermute(x, "dh", [(i, (i + s) % n) for i in range(n)])
    return None


def per_device(hidden_states, norm_gain, head_weight, target_ids, loss_mask, seq_lengths, slot_order):
    rb, dt = hidden_states.shape
    nt = lax.axis_size("t")
    n = lax.axis_size("dh")
    nd = n * 4
    d = dt * nt
    cb = head_weight.shape[1]
    t = lax.axis_index("t")
    dh = lax.axis_index("dh")
    p = lax.axis_index("p")
    dl = lax.axis_index("dl")
    b = (dh * 2 + p) * 2 + dl

    w_p = swap(head_weight, "p")
    block_of = jnp.stack([b, (dh * 2 + 1 - p) * 2 + dl, (dh * 2 + p) * 2 + 1 - dl, (dh * 2 + 1 - p) * 2 + 1 - dl])
    column = ((t * nd + block_of)[:, None] * cb + jnp.arange(cb, dtype=jnp.int32)[None, :]).reshape(-1)

    gain = norm_gain.astype(jnp.float32)
    if n > 4:
        gathered_h = lax.all_gather(hidden_states, "dh", axis=0, tiled=False)
        gathered_t = lax.all_gather(target_ids, "dh", axis=0, tiled=False)

    else:
        extra = (2 * rb) // dt if (2 * rb) % dt == 0 else 0
        if extra:
            code = jnp.concatenate([target_ids // 128, target_ids % 128]).astype(jnp.bfloat16).reshape(extra, dt)
            carried = jnp.concatenate([hidden_states, code], 0)
            moved = [shifted(carried, s, n, dh) for s in range(1, n)]
            moved_t = []
        else:
            moved = [shifted(hidden_states, s, n, dh) for s in range(1, n)]
            moved_t = [shifted(target_ids, s, n, dh) for s in range(1, n)]
        own_other = swap(hidden_states, "t") if nt == 2 else hidden_states
        w_c = swap(head_weight, "dl")
        w_p, w_c, own_other, moved, moved_t = lax.optimization_barrier((w_p, w_c, own_other, moved, moved_t))
        if extra:
            moved_t = []
            for block in moved:
                parts = block[rb:].reshape(2, rb).astype(jnp.int32)
                moved_t.append(parts[0] * 128 + parts[1])
            moved = [block[:rb] for block in moved]

    def normalize(values):
        values = values.astype(jnp.float32)
        square = jnp.mean(values * values, axis=1, keepdims=True)
        return (values * lax.rsqrt(square + EPS) * gain[None, :]).astype(jnp.bfloat16)

    def block_stats(values, t_s, w_all, col=None):
        col = column if col is None else col
        logits = jnp.dot(normalize(values), w_all, preferred_element_type=jnp.float32)
        top = jnp.max(logits, axis=1)
        shift = logits - top[:, None]
        expo = jnp.exp(shift)
        total = jnp.sum(expo, axis=1)
        spread = jnp.sum(expo * shift, axis=1)
        picked = jnp.sum(jnp.where(col[None, :] == t_s[:, None], logits, 0.0), axis=1)
        return jnp.stack([top, total, spread, picked])

    def combine(pieces):
        got = jnp.stack(pieces)
        tops, totals, spreads, pickeds = got[:, 0], got[:, 1], got[:, 2], got[:, 3]
        top = jnp.max(tops, axis=0)
        scale = jnp.exp(tops - top[None, :])
        total = jnp.sum(totals * scale, axis=0)
        spread = jnp.sum(scale * (spreads + totals * (tops - top[None, :])), axis=0)
        return jnp.stack([top, total, spread, jnp.sum(pickeds, axis=0)])

    def joined(x, other):
        return jnp.where(t == 0, jnp.concatenate([x, other], 1), jnp.concatenate([other, x], 1))

    stats = []
    if n <= 4 and nt == 2:
        cols = [column[i * cb:(i + 1) * cb] for i in range(4)]
        w_d = swap(w_p, "dl")
        early = [(head_weight, cols[0]), (w_p, cols[1]), (w_c, cols[2])]
        other = {}
        values = joined(hidden_states, own_other)
        first = [block_stats(values, target_ids, w, c) for w, c in early]
        if n > 1:
            first, w_d, other[1] = lax.optimization_barrier((first, w_d, swap(moved[0], "t")))
        else:
            first, w_d = lax.optimization_barrier((first, w_d))
        pieces_w = early + [(w_d, cols[3])]
        for s in range(n):
            if s == 0:
                block = combine(first + [block_stats(values, target_ids, w_d, cols[3])])
            else:
                values_s = joined(moved[s - 1], other[s])
                block = combine([block_stats(values_s, moved_t[s - 1], w, c) for w, c in pieces_w])
            if s + 2 < n:
                block, other[s + 2] = lax.optimization_barrier((block, swap(moved[s + 1], "t")))
            stats.append(block)
    else:
        w_pair = jnp.concatenate([head_weight, w_p], 1)
        w_all = jnp.concatenate([w_pair, swap(w_pair, "dl")], 1)
        for s in range(n):
            if n > 4:
                src = (dh - s) % n
                h_s, t_s = gathered_h[src], gathered_t[src]
                values = whole_rows(h_s, t, nt)
            elif s == 0:
                h_s, t_s = hidden_states, target_ids
                values = whole_rows(h_s, t, nt)
            else:
                h_s, t_s = moved[s - 1], moved_t[s - 1]
                values = whole_rows(h_s, t, nt)
            stats.append(block_stats(values, t_s, w_all))
    stats = jnp.stack(stats)
    stats = jnp.take(stats, (dh - jnp.arange(n)) % n, axis=0)
    rq = rb // nt
    stats = stats.reshape(n, 4, nt, rq).transpose(0, 2, 1, 3).reshape(n * nt, 4, rq)
    got = lax.all_to_all(stats, ("dh", "t"), 0, 0, tiled=True)
    tops, totals, spreads, pickeds = got[:, 0], got[:, 1], got[:, 2], got[:, 3]
    row_top = jnp.max(tops, axis=0)
    scale = jnp.exp(tops - row_top[None, :])
    row_total = jnp.sum(totals * scale, axis=0)
    row_spread = jnp.sum(scale * (spreads + totals * (tops - row_top[None, :])), axis=0)
    row_picked = jnp.sum(pickeds, axis=0)

    logsum = jnp.log(row_total)
    live = lax.dynamic_slice_in_dim(loss_mask, t * rq, rq).astype(jnp.float32)
    token_logprob = (row_picked - row_top - logsum) * live
    token_entropy = (logsum - row_spread / row_total) * live

    seqs = slot_order.shape[0]
    ends = jnp.cumsum(seq_lengths)
    position = b * rb + t * rq + jnp.arange(rq, dtype=jnp.int32)
    segment = jnp.sum((position[:, None] >= ends[None, :]).astype(jnp.int32), axis=1)
    member = (segment[:, None] == slot_order[None, :]).astype(jnp.float32)
    lp_part = jnp.dot(token_logprob, member, precision=lax.Precision.HIGHEST)
    ent_part = jnp.dot(token_entropy, member, precision=lax.Precision.HIGHEST)
    count_part = jnp.dot(live, member, precision=lax.Precision.HIGHEST)
    k = seqs // nd
    parts = jnp.stack([lp_part, ent_part, count_part]).reshape(3, nd, k).transpose(1, 0, 2)
    parts = jnp.broadcast_to(parts[:, None], (nd, nt, 3, k)).reshape(nd * nt, 3, k)
    sums = jnp.sum(lax.all_to_all(parts, ALL, 0, 0, tiled=True), axis=0)
    floor = jnp.maximum(sums[2], 1.0)
    return (token_logprob, token_entropy, sums[0] / floor, sums[1] / floor)


def solution(mesh):
    nd, nt = mesh.devices.shape
    grid = Mesh(mesh.devices.reshape(nd // 4, 2, 2, nt), ALL)
    placed = (P(ROWS, "t"), P(), P(None, ("t",) + ROWS), P(ROWS), P(ROWS), P(), P())
    return jax.shard_map(
        per_device,
        mesh=grid,
        in_specs=placed,
        out_specs=(P(ALL), P(ALL), P(ROWS), P(ROWS)),
        check_vma=False,
    )
```

```python
import jax
import jax.numpy as jnp
import numpy as np
from jax import lax
from jax.sharding import Mesh
from jax.sharding import PartitionSpec as P

EPS = 1e-05
ROWS = ("dh", "p", "dl")
ALL = ("dh", "p", "dl", "t")


def swap(x, name):
    return lax.ppermute(x, name, [(0, 1), (1, 0)])


def whole_rows(x, t, nt, other=None):
    if nt == 2:
        if other is None:
            other = swap(x, "t")
        return jnp.where(t == 0, jnp.concatenate([x, other], 1), jnp.concatenate([other, x], 1))
    return lax.all_gather(x, "t", axis=1, tiled=True)


def shifted(x, s, n, dh):
    if s == 0:
        return x
    if n <= 4:
        return lax.ppermute(x, "dh", [(i, (i + s) % n) for i in range(n)])
    return None


def per_device(hidden_states, norm_gain, head_weight, target_ids, loss_mask, seq_lengths, slot_order):
    rb, dt = hidden_states.shape
    nt = lax.axis_size("t")
    n = lax.axis_size("dh")
    nd = n * 4
    d = dt * nt
    cb = head_weight.shape[1]
    t = lax.axis_index("t")
    dh = lax.axis_index("dh")
    p = lax.axis_index("p")
    dl = lax.axis_index("dl")
    b = (dh * 2 + p) * 2 + dl

    w_p = swap(head_weight, "p")
    block_of = jnp.stack([b, (dh * 2 + 1 - p) * 2 + dl, (dh * 2 + p) * 2 + 1 - dl, (dh * 2 + 1 - p) * 2 + 1 - dl])
    column = ((t * nd + block_of)[:, None] * cb + jnp.arange(cb, dtype=jnp.int32)[None, :]).reshape(-1)

    gain = norm_gain.astype(jnp.float32)
    if n > 4:
        gathered_h = lax.all_gather(hidden_states, "dh", axis=0, tiled=False)
        gathered_t = lax.all_gather(target_ids, "dh", axis=0, tiled=False)

    else:
        fast = nt == 2 and (2 * rb) % dt == 0
        if not fast:
            moved = [shifted(hidden_states, s, n, dh) for s in range(1, n)]
            moved_t = [shifted(target_ids, s, n, dh) for s in range(1, n)]
            w_p, moved, moved_t = lax.optimization_barrier((w_p, moved, moved_t))

    def normalize(values):
        values = values.astype(jnp.float32)
        square = jnp.mean(values * values, axis=1, keepdims=True)
        return (values * lax.rsqrt(square + EPS) * gain[None, :]).astype(jnp.bfloat16)

    def block_stats(values, t_s, w_all, col=None):
        col = column if col is None else col
        logits = jnp.dot(normalize(values), w_all, preferred_element_type=jnp.float32)
        top = jnp.max(logits, axis=1)
        shift = logits - top[:, None]
        expo = jnp.exp(shift)
        total = jnp.sum(expo, axis=1)
        spread = jnp.sum(expo * shift, axis=1)
        picked = jnp.sum(jnp.where(col[None, :] == t_s[:, None], logits, 0.0), axis=1)
        return jnp.stack([top, total, spread, picked])

    def combine(pieces):
        got = jnp.stack(pieces)
        tops, totals, spreads, pickeds = got[:, 0], got[:, 1], got[:, 2], got[:, 3]
        top = jnp.max(tops, axis=0)
        scale = jnp.exp(tops - top[None, :])
        total = jnp.sum(totals * scale, axis=0)
        spread = jnp.sum(scale * (spreads + totals * (tops - top[None, :])), axis=0)
        return jnp.stack([top, total, spread, jnp.sum(pickeds, axis=0)])

    def joined(x, other):
        return jnp.where(t == 0, jnp.concatenate([x, other], 1), jnp.concatenate([other, x], 1))

    stats = []
    if n <= 4 and fast:
        extra = (2 * rb) // dt
        code = jnp.concatenate([target_ids // 128, target_ids % 128]).astype(jnp.bfloat16).reshape(extra, dt)
        carried = jnp.concatenate([hidden_states, code], 0)
        near = [s for s in sorted({1, n - 1}) if 1 <= s < n]
        far = [s for s in range(1, n) if s not in near]
        cols = [column[i * cb:(i + 1) * cb] for i in range(4)]

        def unpack(block):
            parts = block[rb:].reshape(2, rb).astype(jnp.int32)
            return block[:rb], parts[0] * 128 + parts[1]

        own_other, w_c, got = lax.optimization_barrier(
            (swap(hidden_states, "t"), swap(head_weight, "dl"), [shifted(carried, s, n, dh) for s in near]))
        rows = {0: (hidden_states, target_ids)}
        for s, block in zip(near, got):
            rows[s] = unpack(block)
        values = {0: joined(hidden_states, own_other)}
        first = [block_stats(values[0], target_ids, w, c) for w, c in ((head_weight, cols[0]), (w_c, cols[2]), (w_p, cols[1]))]
        first, got, others = lax.optimization_barrier(
            (first, [shifted(carried, s, n, dh) for s in far], [swap(rows[s][0], "t") for s in near]))
        for s, block in zip(far, got):
            rows[s] = unpack(block)
        for s, other in zip(near, others):
            values[s] = joined(rows[s][0], other)
        early = {s: [block_stats(values[s], rows[s][1], w, c) for w, c in ((head_weight, cols[0]), (w_c, cols[2]), (w_p, cols[1]))] for s in near}
        early, w_d, others = lax.optimization_barrier(
            (early, swap(w_p, "dl"), [swap(rows[s][0], "t") for s in far]))
        for s, other in zip(far, others):
            values[s] = joined(rows[s][0], other)
        early[0] = first
        pieces = ((head_weight, cols[0]), (w_c, cols[2]), (w_p, cols[1]), (w_d, cols[3]))
        for s in range(n):
            if s in early:
                parts = early[s] + [block_stats(values[s], rows[s][1], w_d, cols[3])]
            else:
                parts = [block_stats(values[s], rows[s][1], w, c) for w, c in pieces]
            stats.append(combine(parts))
    else:
        w_pair = jnp.concatenate([head_weight, w_p], 1)
        w_all = jnp.concatenate([w_pair, swap(w_pair, "dl")], 1)
        for s in range(n):
            if n > 4:
                src = (dh - s) % n
                h_s, t_s = gathered_h[src], gathered_t[src]
                values = whole_rows(h_s, t, nt)
            elif s == 0:
                h_s, t_s = hidden_states, target_ids
                values = whole_rows(h_s, t, nt)
            else:
                h_s, t_s = moved[s - 1], moved_t[s - 1]
                values = whole_rows(h_s, t, nt)
            stats.append(block_stats(values, t_s, w_all))
    stats = jnp.stack(stats)
    stats = jnp.take(stats, (dh - jnp.arange(n)) % n, axis=0)
    rq = rb // nt
    stats = stats.reshape(n, 4, nt, rq).transpose(0, 2, 1, 3).reshape(n * nt, 4, rq)
    got = lax.all_to_all(stats, ("dh", "t"), 0, 0, tiled=True)
    tops, totals, spreads, pickeds = got[:, 0], got[:, 1], got[:, 2], got[:, 3]
    row_top = jnp.max(tops, axis=0)
    scale = jnp.exp(tops - row_top[None, :])
    row_total = jnp.sum(totals * scale, axis=0)
    row_spread = jnp.sum(scale * (spreads + totals * (tops - row_top[None, :])), axis=0)
    row_picked = jnp.sum(pickeds, axis=0)

    logsum = jnp.log(row_total)
    live = lax.dynamic_slice_in_dim(loss_mask, t * rq, rq).astype(jnp.float32)
    token_logprob = (row_picked - row_top - logsum) * live
    token_entropy = (logsum - row_spread / row_total) * live

    seqs = slot_order.shape[0]
    ends = jnp.cumsum(seq_lengths)
    position = b * rb + t * rq + jnp.arange(rq, dtype=jnp.int32)
    segment = jnp.sum((position[:, None] >= ends[None, :]).astype(jnp.int32), axis=1)
    member = (segment[:, None] == slot_order[None, :]).astype(jnp.float32)
    lp_part = jnp.dot(token_logprob, member, precision=lax.Precision.HIGHEST)
    ent_part = jnp.dot(token_entropy, member, precision=lax.Precision.HIGHEST)
    count_part = jnp.dot(live, member, precision=lax.Precision.HIGHEST)
    k = seqs // nd
    parts = jnp.stack([lp_part, ent_part, count_part]).reshape(3, nd, k).transpose(1, 0, 2)
    parts = jnp.broadcast_to(parts[:, None], (nd, nt, 3, k)).reshape(nd * nt, 3, k)
    sums = jnp.sum(lax.all_to_all(parts, ALL, 0, 0, tiled=True), axis=0)
    floor = jnp.maximum(sums[2], 1.0)
    return (token_logprob, token_entropy, sums[0] / floor, sums[1] / floor)


def solution(mesh):
    nd, nt = mesh.devices.shape
    grid = Mesh(mesh.devices.reshape(nd // 4, 2, 2, nt), ALL)
    placed = (P(ROWS, "t"), P(), P(None, ("t",) + ROWS), P(ROWS), P(ROWS), P(), P())
    return jax.shard_map(
        per_device,
        mesh=grid,
        in_specs=placed,
        out_specs=(P(ALL), P(ALL), P(ROWS), P(ROWS)),
        check_vma=False,
    )
```

```python
import jax
import jax.numpy as jnp
import numpy as np
from jax import lax
from jax.sharding import Mesh
from jax.sharding import PartitionSpec as P

EPS = 1e-05
ROWS = ("dh", "p", "dl")
ALL = ("dh", "p", "dl", "t")


def swap(x, name):
    return lax.ppermute(x, name, [(0, 1), (1, 0)])


def whole_rows(x, t, nt, other=None):
    if nt == 2:
        if other is None:
            other = swap(x, "t")
        return jnp.where(t == 0, jnp.concatenate([x, other], 1), jnp.concatenate([other, x], 1))
    return lax.all_gather(x, "t", axis=1, tiled=True)


def shifted(x, s, n, dh):
    if s == 0:
        return x
    if n <= 4:
        return lax.ppermute(x, "dh", [(i, (i + s) % n) for i in range(n)])
    return None


def per_device(hidden_states, norm_gain, head_weight, target_ids, loss_mask, seq_lengths, slot_order):
    rb, dt = hidden_states.shape
    nt = lax.axis_size("t")
    n = lax.axis_size("dh")
    nd = n * 4
    d = dt * nt
    cb = head_weight.shape[1]
    t = lax.axis_index("t")
    dh = lax.axis_index("dh")
    p = lax.axis_index("p")
    dl = lax.axis_index("dl")
    b = (dh * 2 + p) * 2 + dl

    w_p = swap(head_weight, "p")
    block_of = jnp.stack([b, (dh * 2 + 1 - p) * 2 + dl, (dh * 2 + p) * 2 + 1 - dl, (dh * 2 + 1 - p) * 2 + 1 - dl])
    column = ((t * nd + block_of)[:, None] * cb + jnp.arange(cb, dtype=jnp.int32)[None, :]).reshape(-1)

    gain = norm_gain.astype(jnp.float32)
    if n > 4:
        gathered_h = lax.all_gather(hidden_states, "dh", axis=0, tiled=False)
        gathered_t = lax.all_gather(target_ids, "dh", axis=0, tiled=False)

    else:
        fast = nt == 2 and (2 * rb) % dt == 0
        if not fast:
            moved = [shifted(hidden_states, s, n, dh) for s in range(1, n)]
            moved_t = [shifted(target_ids, s, n, dh) for s in range(1, n)]
            w_p, moved, moved_t = lax.optimization_barrier((w_p, moved, moved_t))

    def normalize(values):
        values = values.astype(jnp.float32)
        square = jnp.mean(values * values, axis=1, keepdims=True)
        return (values * lax.rsqrt(square + EPS) * gain[None, :]).astype(jnp.bfloat16)

    def block_stats(values, t_s, w_all, col=None):
        col = column if col is None else col
        logits = jnp.dot(normalize(values), w_all, preferred_element_type=jnp.float32)
        top = jnp.max(logits, axis=1)
        shift = logits - top[:, None]
        expo = jnp.exp(shift)
        total = jnp.sum(expo, axis=1)
        spread = jnp.sum(expo * shift, axis=1)
        picked = jnp.sum(jnp.where(col[None, :] == t_s[:, None], logits, 0.0), axis=1)
        return jnp.stack([top, total, spread, picked])

    def combine(pieces):
        got = jnp.stack(pieces)
        tops, totals, spreads, pickeds = got[:, 0], got[:, 1], got[:, 2], got[:, 3]
        top = jnp.max(tops, axis=0)
        scale = jnp.exp(tops - top[None, :])
        total = jnp.sum(totals * scale, axis=0)
        spread = jnp.sum(scale * (spreads + totals * (tops - top[None, :])), axis=0)
        return jnp.stack([top, total, spread, jnp.sum(pickeds, axis=0)])

    def joined(x, other):
        return jnp.where(t == 0, jnp.concatenate([x, other], 1), jnp.concatenate([other, x], 1))

    stats = []
    if n <= 4 and fast:
        extra = (2 * rb) // dt
        code = jnp.concatenate([target_ids // 128, target_ids % 128]).astype(jnp.bfloat16).reshape(extra, dt)
        carried = jnp.concatenate([hidden_states, code], 0)
        near = [s for s in sorted({1, n - 1}) if 1 <= s < n]
        far = [s for s in range(1, n) if s not in near]
        cols = [column[i * cb:(i + 1) * cb] for i in range(4)]

        def unpack(block):
            parts = block[rb:].reshape(2, rb).astype(jnp.int32)
            return block[:rb], parts[0] * 128 + parts[1]

        own_other, w_c, got = lax.optimization_barrier(
            (swap(hidden_states, "t"), swap(head_weight, "dl"), [shifted(carried, s, n, dh) for s in near]))
        rows = {0: (hidden_states, target_ids)}
        for s, block in zip(near, got):
            rows[s] = unpack(block)
        values = {0: joined(hidden_states, own_other)}
        w_own = jnp.concatenate([head_weight, w_c], 1)
        c_own = jnp.concatenate([cols[0], cols[2]])
        held = ((w_own, c_own), (w_p, cols[1]))
        first = [block_stats(values[0], target_ids, w, c) for w, c in held]
        first, got, others = lax.optimization_barrier(
            (first, [shifted(carried, s, n, dh) for s in far], [swap(rows[s][0], "t") for s in near]))
        for s, block in zip(far, got):
            rows[s] = unpack(block)
        for s, other in zip(near, others):
            values[s] = joined(rows[s][0], other)
        early = {0: first}
        lead = near[0] if near else None
        lead_stats = [block_stats(values[lead], rows[lead][1], w, c) for w, c in held] if near else []
        lead_stats, w_d, others = lax.optimization_barrier(
            (lead_stats, swap(w_p, "dl"), [swap(rows[s][0], "t") for s in far]))
        if near:
            early[lead] = lead_stats
        for s, other in zip(far, others):
            values[s] = joined(rows[s][0], other)
        for s in near[1:]:
            early[s] = [block_stats(values[s], rows[s][1], w, c) for w, c in held]
        pieces = held + ((w_d, cols[3]),)
        for s in range(n):
            if s in early:
                parts = early[s] + [block_stats(values[s], rows[s][1], w_d, cols[3])]
            else:
                parts = [block_stats(values[s], rows[s][1], w, c) for w, c in pieces]
            stats.append(combine(parts))
    else:
        w_pair = jnp.concatenate([head_weight, w_p], 1)
        w_all = jnp.concatenate([w_pair, swap(w_pair, "dl")], 1)
        for s in range(n):
            if n > 4:
                src = (dh - s) % n
                h_s, t_s = gathered_h[src], gathered_t[src]
                values = whole_rows(h_s, t, nt)
            elif s == 0:
                h_s, t_s = hidden_states, target_ids
                values = whole_rows(h_s, t, nt)
            else:
                h_s, t_s = moved[s - 1], moved_t[s - 1]
                values = whole_rows(h_s, t, nt)
            stats.append(block_stats(values, t_s, w_all))
    stats = jnp.stack(stats)
    stats = jnp.take(stats, (dh - jnp.arange(n)) % n, axis=0)
    rq = rb // nt
    stats = stats.reshape(n, 4, nt, rq).transpose(0, 2, 1, 3).reshape(n * nt, 4, rq)
    got = lax.all_to_all(stats, ("dh", "t"), 0, 0, tiled=True)
    tops, totals, spreads, pickeds = got[:, 0], got[:, 1], got[:, 2], got[:, 3]
    row_top = jnp.max(tops, axis=0)
    scale = jnp.exp(tops - row_top[None, :])
    row_total = jnp.sum(totals * scale, axis=0)
    row_spread = jnp.sum(scale * (spreads + totals * (tops - row_top[None, :])), axis=0)
    row_picked = jnp.sum(pickeds, axis=0)

    logsum = jnp.log(row_total)
    live = lax.dynamic_slice_in_dim(loss_mask, t * rq, rq).astype(jnp.float32)
    token_logprob = (row_picked - row_top - logsum) * live
    token_entropy = (logsum - row_spread / row_total) * live

    seqs = slot_order.shape[0]
    ends = jnp.cumsum(seq_lengths)
    position = b * rb + t * rq + jnp.arange(rq, dtype=jnp.int32)
    segment = jnp.sum((position[:, None] >= ends[None, :]).astype(jnp.int32), axis=1)
    member = (segment[:, None] == slot_order[None, :]).astype(jnp.float32)
    lp_part = jnp.dot(token_logprob, member, precision=lax.Precision.HIGHEST)
    ent_part = jnp.dot(token_entropy, member, precision=lax.Precision.HIGHEST)
    count_part = jnp.dot(live, member, precision=lax.Precision.HIGHEST)
    k = seqs // nd
    parts = jnp.stack([lp_part, ent_part, count_part]).reshape(3, nd, k).transpose(1, 0, 2)
    parts = jnp.broadcast_to(parts[:, None], (nd, nt, 3, k)).reshape(nd * nt, 3, k)
    sums = jnp.sum(lax.all_to_all(parts, ALL, 0, 0, tiled=True), axis=0)
    floor = jnp.maximum(sums[2], 1.0)
    return (token_logprob, token_entropy, sums[0] / floor, sums[1] / floor)


def solution(mesh):
    nd, nt = mesh.devices.shape
    grid = Mesh(mesh.devices.reshape(nd // 4, 2, 2, nt), ALL)
    placed = (P(ROWS, "t"), P(), P(None, ("t",) + ROWS), P(ROWS), P(ROWS), P(), P())
    return jax.shard_map(
        per_device,
        mesh=grid,
        in_specs=placed,
        out_specs=(P(ALL), P(ALL), P(ROWS), P(ROWS)),
        check_vma=False,
    )
```

```python
import jax
import jax.numpy as jnp
import numpy as np
from jax import lax
from jax.sharding import Mesh
from jax.sharding import PartitionSpec as P

EPS = 1e-05
ROWS = ("dh", "p", "dl")
ALL = ("dh", "p", "dl", "t")


def swap(x, name):
    return lax.ppermute(x, name, [(0, 1), (1, 0)])


def whole_rows(x, t, nt, other=None):
    if nt == 2:
        if other is None:
            other = swap(x, "t")
        return jnp.where(t == 0, jnp.concatenate([x, other], 1), jnp.concatenate([other, x], 1))
    return lax.all_gather(x, "t", axis=1, tiled=True)


def shifted(x, s, n, dh):
    if s == 0:
        return x
    if n <= 4:
        return lax.ppermute(x, "dh", [(i, (i + s) % n) for i in range(n)])
    return None


def per_device(hidden_states, norm_gain, head_weight, target_ids, loss_mask, seq_lengths, slot_order):
    rb, dt = hidden_states.shape
    nt = lax.axis_size("t")
    n = lax.axis_size("dh")
    nd = n * 4
    d = dt * nt
    cb = head_weight.shape[1]
    t = lax.axis_index("t")
    dh = lax.axis_index("dh")
    p = lax.axis_index("p")
    dl = lax.axis_index("dl")
    b = (dh * 2 + p) * 2 + dl

    w_p = swap(head_weight, "p")
    block_of = jnp.stack([b, (dh * 2 + 1 - p) * 2 + dl, (dh * 2 + p) * 2 + 1 - dl, (dh * 2 + 1 - p) * 2 + 1 - dl])
    column = ((t * nd + block_of)[:, None] * cb + jnp.arange(cb, dtype=jnp.int32)[None, :]).reshape(-1)

    gain = norm_gain.astype(jnp.float32)
    if n > 4:
        gathered_h = lax.all_gather(hidden_states, "dh", axis=0, tiled=False)
        gathered_t = lax.all_gather(target_ids, "dh", axis=0, tiled=False)

    else:
        fast = nt == 2 and (2 * rb) % dt == 0
        if not fast:
            moved = [shifted(hidden_states, s, n, dh) for s in range(1, n)]
            moved_t = [shifted(target_ids, s, n, dh) for s in range(1, n)]
            w_p, moved, moved_t = lax.optimization_barrier((w_p, moved, moved_t))

    def normalize(values):
        values = values.astype(jnp.float32)
        square = jnp.mean(values * values, axis=1, keepdims=True)
        return (values * lax.rsqrt(square + EPS) * gain[None, :]).astype(jnp.bfloat16)

    def block_stats(values, t_s, w_all, col=None):
        col = column if col is None else col
        logits = jnp.dot(normalize(values), w_all, preferred_element_type=jnp.float32)
        top = jnp.max(logits, axis=1)
        shift = logits - top[:, None]
        expo = jnp.exp(shift)
        total = jnp.sum(expo, axis=1)
        spread = jnp.sum(expo * shift, axis=1)
        picked = jnp.sum(jnp.where(col[None, :] == t_s[:, None], logits, 0.0), axis=1)
        return jnp.stack([top, total, spread, picked])

    def combine(pieces):
        got = jnp.stack(pieces)
        tops, totals, spreads, pickeds = got[:, 0], got[:, 1], got[:, 2], got[:, 3]
        top = jnp.max(tops, axis=0)
        scale = jnp.exp(tops - top[None, :])
        total = jnp.sum(totals * scale, axis=0)
        spread = jnp.sum(scale * (spreads + totals * (tops - top[None, :])), axis=0)
        return jnp.stack([top, total, spread, jnp.sum(pickeds, axis=0)])

    def joined(x, other):
        return jnp.where(t == 0, jnp.concatenate([x, other], 1), jnp.concatenate([other, x], 1))

    stats = []
    if n <= 4 and fast:
        extra = (2 * rb) // dt
        code = jnp.concatenate([target_ids // 128, target_ids % 128]).astype(jnp.bfloat16).reshape(extra, dt)
        carried = jnp.concatenate([hidden_states, code], 0)
        near = [s for s in sorted({1, n - 1}) if 1 <= s < n]
        far = [s for s in range(1, n) if s not in near]
        cols = [column[i * cb:(i + 1) * cb] for i in range(4)]

        def unpack(block):
            parts = block[rb:].reshape(2, rb).astype(jnp.int32)
            return block[:rb], parts[0] * 128 + parts[1]

        own_other, w_c, got = lax.optimization_barrier(
            (swap(hidden_states, "t"), swap(head_weight, "dl"), [shifted(carried, s, n, dh) for s in near]))
        rows = {0: (hidden_states, target_ids)}
        for s, block in zip(near, got):
            rows[s] = unpack(block)
        values = {0: joined(hidden_states, own_other)}
        w_own = jnp.concatenate([head_weight, w_c], 1)
        c_own = jnp.concatenate([cols[0], cols[2]])
        held = ((w_own, c_own), (w_p, cols[1]))
        first = [block_stats(values[0], target_ids, w, c) for w, c in held]
        first, got, others = lax.optimization_barrier(
            (first, [shifted(carried, s, n, dh) for s in far], [swap(rows[s][0], "t") for s in near]))
        for s, block in zip(far, got):
            rows[s] = unpack(block)
        for s, other in zip(near, others):
            values[s] = joined(rows[s][0], other)
        early = {0: first}
        lead = near[0] if near else None
        lead_stats = [block_stats(values[lead], rows[lead][1], w, c) for w, c in held] if near else []
        lead_stats, w_d, others = lax.optimization_barrier(
            (lead_stats, swap(w_p, "dl"), [swap(rows[s][0], "t") for s in far]))
        if near:
            early[lead] = lead_stats
        for s, other in zip(far, others):
            values[s] = joined(rows[s][0], other)
        for s in near[1:]:
            early[s] = [block_stats(values[s], rows[s][1], w, c) for w, c in held]
        pieces = held + ((w_d, cols[3]),)
        for s in range(n):
            if s in early:
                parts = early[s] + [block_stats(values[s], rows[s][1], w_d, cols[3])]
            else:
                parts = [block_stats(values[s], rows[s][1], w, c) for w, c in pieces]
            stats.append(combine(parts))
    else:
        w_pair = jnp.concatenate([head_weight, w_p], 1)
        w_all = jnp.concatenate([w_pair, swap(w_pair, "dl")], 1)
        for s in range(n):
            if n > 4:
                src = (dh - s) % n
                h_s, t_s = gathered_h[src], gathered_t[src]
                values = whole_rows(h_s, t, nt)
            elif s == 0:
                h_s, t_s = hidden_states, target_ids
                values = whole_rows(h_s, t, nt)
            else:
                h_s, t_s = moved[s - 1], moved_t[s - 1]
                values = whole_rows(h_s, t, nt)
            stats.append(block_stats(values, t_s, w_all))
    stats = jnp.stack(stats)
    stats = jnp.take(stats, (dh - jnp.arange(n)) % n, axis=0)
    rq = rb // nt
    stats = stats.reshape(n, 4, nt, rq).transpose(0, 2, 1, 3).reshape(n * nt, 4, rq)
    got = lax.all_to_all(stats, ("dh", "t"), 0, 0, tiled=True)
    tops, totals, spreads, pickeds = got[:, 0], got[:, 1], got[:, 2], got[:, 3]
    row_top = jnp.max(tops, axis=0)
    scale = jnp.exp(tops - row_top[None, :])
    row_total = jnp.sum(totals * scale, axis=0)
    row_spread = jnp.sum(scale * (spreads + totals * (tops - row_top[None, :])), axis=0)
    row_picked = jnp.sum(pickeds, axis=0)

    logsum = jnp.log(row_total)
    live = lax.dynamic_slice_in_dim(loss_mask, t * rq, rq).astype(jnp.float32)
    token_logprob = (row_picked - row_top - logsum) * live
    token_entropy = (logsum - row_spread / row_total) * live

    seqs = slot_order.shape[0]
    ends = jnp.cumsum(seq_lengths)
    position = b * rb + t * rq + jnp.arange(rq, dtype=jnp.int32)
    segment = jnp.sum((position[:, None] >= ends[None, :]).astype(jnp.int32), axis=1)
    member = segment[:, None] == slot_order[None, :]
    rowwise = jnp.stack([token_logprob, token_entropy, live])
    k = seqs // nd
    parts = jnp.sum(jnp.where(member[None], rowwise[:, :, None], 0.0), axis=1)
    parts = parts.reshape(3, nd, k).transpose(1, 0, 2)
    parts = jnp.broadcast_to(parts[:, None], (nd, nt, 3, k)).reshape(nd * nt, 3, k)
    sums = jnp.sum(lax.all_to_all(parts, ALL, 0, 0, tiled=True), axis=0)
    floor = jnp.maximum(sums[2], 1.0)
    return (token_logprob, token_entropy, sums[0] / floor, sums[1] / floor)


def solution(mesh):
    nd, nt = mesh.devices.shape
    grid = Mesh(mesh.devices.reshape(nd // 4, 2, 2, nt), ALL)
    placed = (P(ROWS, "t"), P(), P(None, ("t",) + ROWS), P(ROWS), P(ROWS), P(), P())
    return jax.shard_map(
        per_device,
        mesh=grid,
        in_specs=placed,
        out_specs=(P(ALL), P(ALL), P(ROWS), P(ROWS)),
        check_vma=False,
    )
```

```python
import jax
import jax.numpy as jnp
import numpy as np
from jax import lax
from jax.sharding import Mesh
from jax.sharding import PartitionSpec as P

EPS = 1e-05
ROWS = ("dh", "p", "dl")
ALL = ("dh", "p", "dl", "t")


def swap(x, name):
    return lax.ppermute(x, name, [(0, 1), (1, 0)])


def whole_rows(x, t, nt, other=None):
    if nt == 2:
        if other is None:
            other = swap(x, "t")
        return jnp.where(t == 0, jnp.concatenate([x, other], 1), jnp.concatenate([other, x], 1))
    return lax.all_gather(x, "t", axis=1, tiled=True)


def shifted(x, s, n, dh):
    if s == 0:
        return x
    if n <= 4:
        return lax.ppermute(x, "dh", [(i, (i + s) % n) for i in range(n)])
    return None


def per_device(hidden_states, norm_gain, head_weight, target_ids, loss_mask, seq_lengths, slot_order):
    rb, dt = hidden_states.shape
    nt = lax.axis_size("t")
    n = lax.axis_size("dh")
    nd = n * 4
    d = dt * nt
    cb = head_weight.shape[1]
    t = lax.axis_index("t")
    dh = lax.axis_index("dh")
    p = lax.axis_index("p")
    dl = lax.axis_index("dl")
    b = (dh * 2 + p) * 2 + dl

    w_p = swap(head_weight, "p")
    block_of = jnp.stack([b, (dh * 2 + 1 - p) * 2 + dl, (dh * 2 + p) * 2 + 1 - dl, (dh * 2 + 1 - p) * 2 + 1 - dl])
    column = ((t * nd + block_of)[:, None] * cb + jnp.arange(cb, dtype=jnp.int32)[None, :]).reshape(-1)

    gain = norm_gain.astype(jnp.float32)
    if n > 4:
        gathered_h = lax.all_gather(hidden_states, "dh", axis=0, tiled=False)
        gathered_t = lax.all_gather(target_ids, "dh", axis=0, tiled=False)

    else:
        fast = nt == 2 and (2 * rb) % dt == 0
        if not fast:
            moved = [shifted(hidden_states, s, n, dh) for s in range(1, n)]
            moved_t = [shifted(target_ids, s, n, dh) for s in range(1, n)]
            w_p, moved, moved_t = lax.optimization_barrier((w_p, moved, moved_t))

    def normalize(values):
        values = values.astype(jnp.float32)
        square = jnp.mean(values * values, axis=1, keepdims=True)
        return (values * lax.rsqrt(square + EPS) * gain[None, :]).astype(jnp.bfloat16)

    def block_stats(values, t_s, w_all, col=None):
        return logit_stats(jnp.dot(normalize(values), w_all, preferred_element_type=jnp.float32), t_s, col)

    def logit_stats(logits, t_s, col=None):
        col = column if col is None else col
        top = jnp.max(logits, axis=1)
        shift = logits - top[:, None]
        expo = jnp.exp(shift)
        total = jnp.sum(expo, axis=1)
        spread = jnp.sum(expo * shift, axis=1)
        picked = jnp.sum(jnp.where(col[None, :] == t_s[:, None], logits, 0.0), axis=1)
        return jnp.stack([top, total, spread, picked])

    def combine(pieces):
        got = jnp.stack(pieces)
        tops, totals, spreads, pickeds = got[:, 0], got[:, 1], got[:, 2], got[:, 3]
        top = jnp.max(tops, axis=0)
        scale = jnp.exp(tops - top[None, :])
        total = jnp.sum(totals * scale, axis=0)
        spread = jnp.sum(scale * (spreads + totals * (tops - top[None, :])), axis=0)
        return jnp.stack([top, total, spread, jnp.sum(pickeds, axis=0)])

    def joined(x, other):
        return jnp.where(t == 0, jnp.concatenate([x, other], 1), jnp.concatenate([other, x], 1))

    stats = []
    if n <= 4 and fast:
        extra = (2 * rb) // dt
        code = jnp.concatenate([target_ids // 128, target_ids % 128]).astype(jnp.bfloat16).reshape(extra, dt)
        carried = jnp.concatenate([hidden_states, code], 0)
        near = [s for s in sorted({1, n - 1}) if 1 <= s < n]
        far = [s for s in range(1, n) if s not in near]
        cols = [column[i * cb:(i + 1) * cb] for i in range(4)]

        def unpack(block):
            parts = block[rb:].reshape(2, rb).astype(jnp.int32)
            return block[:rb], parts[0] * 128 + parts[1]

        own_other, w_c, got = lax.optimization_barrier(
            (swap(hidden_states, "t"), swap(head_weight, "dl"), [shifted(carried, s, n, dh) for s in near]))
        rows = {0: (hidden_states, target_ids)}
        for s, block in zip(near, got):
            rows[s] = unpack(block)
        values = {0: joined(hidden_states, own_other)}
        w_own = jnp.concatenate([head_weight, w_c], 1)
        c_own = jnp.concatenate([cols[0], cols[2]])
        held = ((w_own, c_own), (w_p, cols[1]))
        values0 = values[0].astype(jnp.float32)
        factor = lax.rsqrt(jnp.mean(values0 * values0, axis=1) + EPS)
        first = [block_stats(values[0], target_ids, w, c) for w, c in held]

        def half_dot(x, f, half, w):
            g = lax.dynamic_slice_in_dim(gain, half * dt, dt)
            normed = (x.astype(jnp.float32) * f[:, None] * g[None, :]).astype(jnp.bfloat16)
            return jnp.dot(normed, lax.dynamic_slice_in_dim(w, half * dt, dt, axis=0), preferred_element_type=jnp.float32)

        factors = {s: shifted(factor, s, n, dh) for s in near}
        partial = {s: [half_dot(rows[s][0], factors[s], t, w) for w, _ in held] for s in near}
        first, partial, got, others = lax.optimization_barrier(
            (first, partial, [shifted(carried, s, n, dh) for s in far], [swap(rows[s][0], "t") for s in near]))
        for s, block in zip(far, got):
            rows[s] = unpack(block)
        swapped = dict(zip(near, others))
        for s, other in swapped.items():
            values[s] = joined(rows[s][0], other)

        def near_stats(s):
            other = swapped[s]
            return [logit_stats(part + half_dot(other, factors[s], 1 - t, w), rows[s][1], c)
                    for part, (w, c) in zip(partial[s], held)]

        early = {0: first}
        lead = near[0] if near else None
        lead_stats = near_stats(lead) if near else []
        lead_stats, w_d, others = lax.optimization_barrier(
            (lead_stats, swap(w_p, "dl"), [swap(rows[s][0], "t") for s in far]))
        if near:
            early[lead] = lead_stats
        for s, other in zip(far, others):
            values[s] = joined(rows[s][0], other)
        for s in near[1:]:
            early[s] = near_stats(s)
        pieces = held + ((w_d, cols[3]),)
        for s in range(n):
            if s in early:
                parts = early[s] + [block_stats(values[s], rows[s][1], w_d, cols[3])]
            else:
                parts = [block_stats(values[s], rows[s][1], w, c) for w, c in pieces]
            stats.append(combine(parts))
    else:
        w_pair = jnp.concatenate([head_weight, w_p], 1)
        w_all = jnp.concatenate([w_pair, swap(w_pair, "dl")], 1)
        for s in range(n):
            if n > 4:
                src = (dh - s) % n
                h_s, t_s = gathered_h[src], gathered_t[src]
                values = whole_rows(h_s, t, nt)
            elif s == 0:
                h_s, t_s = hidden_states, target_ids
                values = whole_rows(h_s, t, nt)
            else:
                h_s, t_s = moved[s - 1], moved_t[s - 1]
                values = whole_rows(h_s, t, nt)
            stats.append(block_stats(values, t_s, w_all))
    stats = jnp.stack(stats)
    stats = jnp.take(stats, (dh - jnp.arange(n)) % n, axis=0)
    rq = rb // nt
    stats = stats.reshape(n, 4, nt, rq).transpose(0, 2, 1, 3).reshape(n * nt, 4, rq)
    got = lax.all_to_all(stats, ("dh", "t"), 0, 0, tiled=True)
    tops, totals, spreads, pickeds = got[:, 0], got[:, 1], got[:, 2], got[:, 3]
    row_top = jnp.max(tops, axis=0)
    scale = jnp.exp(tops - row_top[None, :])
    row_total = jnp.sum(totals * scale, axis=0)
    row_spread = jnp.sum(scale * (spreads + totals * (tops - row_top[None, :])), axis=0)
    row_picked = jnp.sum(pickeds, axis=0)

    logsum = jnp.log(row_total)
    live = lax.dynamic_slice_in_dim(loss_mask, t * rq, rq).astype(jnp.float32)
    token_logprob = (row_picked - row_top - logsum) * live
    token_entropy = (logsum - row_spread / row_total) * live

    seqs = slot_order.shape[0]
    ends = jnp.cumsum(seq_lengths)
    position = b * rb + t * rq + jnp.arange(rq, dtype=jnp.int32)
    segment = jnp.sum((position[:, None] >= ends[None, :]).astype(jnp.int32), axis=1)
    member = segment[:, None] == slot_order[None, :]
    rowwise = jnp.stack([token_logprob, token_entropy, live])
    k = seqs // nd
    parts = jnp.sum(jnp.where(member[None], rowwise[:, :, None], 0.0), axis=1)
    parts = parts.reshape(3, nd, k).transpose(1, 0, 2)
    parts = jnp.broadcast_to(parts[:, None], (nd, nt, 3, k)).reshape(nd * nt, 3, k)
    sums = jnp.sum(lax.all_to_all(parts, ALL, 0, 0, tiled=True), axis=0)
    floor = jnp.maximum(sums[2], 1.0)
    return (token_logprob, token_entropy, sums[0] / floor, sums[1] / floor)


def solution(mesh):
    nd, nt = mesh.devices.shape
    grid = Mesh(mesh.devices.reshape(nd // 4, 2, 2, nt), ALL)
    placed = (P(ROWS, "t"), P(), P(None, ("t",) + ROWS), P(ROWS), P(ROWS), P(), P())
    return jax.shard_map(
        per_device,
        mesh=grid,
        in_specs=placed,
        out_specs=(P(ALL), P(ALL), P(ROWS), P(ROWS)),
        check_vma=False,
    )
```

```python
import jax
import jax.numpy as jnp
import numpy as np
from jax import lax
from jax.sharding import Mesh
from jax.sharding import PartitionSpec as P

EPS = 1e-05
ROWS = ("dh", "p", "dl")
ALL = ("dh", "p", "dl", "t")


def swap(x, name):
    return lax.ppermute(x, name, [(0, 1), (1, 0)])


def whole_rows(x, t, nt, other=None):
    if nt == 2:
        if other is None:
            other = swap(x, "t")
        return jnp.where(t == 0, jnp.concatenate([x, other], 1), jnp.concatenate([other, x], 1))
    return lax.all_gather(x, "t", axis=1, tiled=True)


def shifted(x, s, n, dh):
    if s == 0:
        return x
    if n <= 4:
        return lax.ppermute(x, "dh", [(i, (i + s) % n) for i in range(n)])
    return None


def per_device(hidden_states, norm_gain, head_weight, target_ids, loss_mask, seq_lengths, slot_order):
    rb, dt = hidden_states.shape
    nt = lax.axis_size("t")
    n = lax.axis_size("dh")
    nd = n * 4
    d = dt * nt
    cb = head_weight.shape[1]
    t = lax.axis_index("t")
    dh = lax.axis_index("dh")
    p = lax.axis_index("p")
    dl = lax.axis_index("dl")
    b = (dh * 2 + p) * 2 + dl

    w_p = swap(head_weight, "p")
    block_of = jnp.stack([b, (dh * 2 + 1 - p) * 2 + dl, (dh * 2 + p) * 2 + 1 - dl, (dh * 2 + 1 - p) * 2 + 1 - dl])
    column = ((t * nd + block_of)[:, None] * cb + jnp.arange(cb, dtype=jnp.int32)[None, :]).reshape(-1)

    gain = norm_gain.astype(jnp.float32)
    if n > 4:
        gathered_h = lax.all_gather(hidden_states, "dh", axis=0, tiled=False)
        gathered_t = lax.all_gather(target_ids, "dh", axis=0, tiled=False)

    else:
        fast = nt == 2 and (2 * rb) % dt == 0
        if not fast:
            moved = [shifted(hidden_states, s, n, dh) for s in range(1, n)]
            moved_t = [shifted(target_ids, s, n, dh) for s in range(1, n)]
            w_p, moved, moved_t = lax.optimization_barrier((w_p, moved, moved_t))

    def normalize(values):
        values = values.astype(jnp.float32)
        square = jnp.mean(values * values, axis=1, keepdims=True)
        return (values * lax.rsqrt(square + EPS) * gain[None, :]).astype(jnp.bfloat16)

    def block_stats(values, t_s, w_all, col=None):
        col = column if col is None else col
        logits = jnp.dot(normalize(values), w_all, preferred_element_type=jnp.float32)
        top = jnp.max(logits, axis=1)
        shift = logits - top[:, None]
        expo = jnp.exp(shift)
        total = jnp.sum(expo, axis=1)
        spread = jnp.sum(expo * shift, axis=1)
        picked = jnp.sum(jnp.where(col[None, :] == t_s[:, None], logits, 0.0), axis=1)
        return jnp.stack([top, total, spread, picked])

    def combine(pieces):
        got = jnp.stack(pieces)
        tops, totals, spreads, pickeds = got[:, 0], got[:, 1], got[:, 2], got[:, 3]
        top = jnp.max(tops, axis=0)
        scale = jnp.exp(tops - top[None, :])
        total = jnp.sum(totals * scale, axis=0)
        spread = jnp.sum(scale * (spreads + totals * (tops - top[None, :])), axis=0)
        return jnp.stack([top, total, spread, jnp.sum(pickeds, axis=0)])

    def joined(x, other):
        return jnp.where(t == 0, jnp.concatenate([x, other], 1), jnp.concatenate([other, x], 1))

    stats = []
    if n <= 4 and fast:
        extra = (2 * rb) // dt
        code = jnp.concatenate([target_ids // 128, target_ids % 128]).astype(jnp.bfloat16).reshape(extra, dt)
        carried = jnp.concatenate([hidden_states, code], 0)
        near = [s for s in sorted({1, n - 1}) if 1 <= s < n]
        far = [s for s in range(1, n) if s not in near]
        cols = [column[i * cb:(i + 1) * cb] for i in range(4)]

        def unpack(block):
            parts = block[rb:].reshape(2, rb).astype(jnp.int32)
            return block[:rb], parts[0] * 128 + parts[1]

        own_other, w_c, got = lax.optimization_barrier(
            (swap(hidden_states, "t"), swap(head_weight, "dl"), [shifted(carried, s, n, dh) for s in near]))
        rows = {0: (hidden_states, target_ids)}
        for s, block in zip(near, got):
            rows[s] = unpack(block)
        values = {0: joined(hidden_states, own_other)}
        w_own = jnp.concatenate([head_weight, w_c], 1)
        c_own = jnp.concatenate([cols[0], cols[2]])
        held = ((w_own, c_own), (w_p, cols[1]))
        first = [block_stats(values[0], target_ids, w, c) for w, c in held]
        pending_far = [shifted(carried, s, n, dh) for s in far]
        early = {}
        if near:
            first, lead_other = lax.optimization_barrier((first, swap(rows[near[0]][0], "t")))
            values[near[0]] = joined(rows[near[0]][0], lead_other)
            lead_stats = [block_stats(values[near[0]], rows[near[0]][1], w, c) for w, c in held]
            lead_stats, rest, got = lax.optimization_barrier(
                (lead_stats, [swap(rows[s][0], "t") for s in near[1:]], pending_far))
            early[near[0]] = lead_stats
            for s, other in zip(near[1:], rest):
                values[s] = joined(rows[s][0], other)
        else:
            first, got = lax.optimization_barrier((first, pending_far))
        early[0] = first
        for s, block in zip(far, got):
            rows[s] = unpack(block)
        later = {s: [block_stats(values[s], rows[s][1], w, c) for w, c in held] for s in near[1:]}
        later, w_d, others = lax.optimization_barrier(
            (later, swap(w_p, "dl"), [swap(rows[s][0], "t") for s in far]))
        early.update(later)
        for s, other in zip(far, others):
            values[s] = joined(rows[s][0], other)
        pieces = held + ((w_d, cols[3]),)
        for s in range(n):
            if s in early:
                parts = early[s] + [block_stats(values[s], rows[s][1], w_d, cols[3])]
            else:
                parts = [block_stats(values[s], rows[s][1], w, c) for w, c in pieces]
            stats.append(combine(parts))
    else:
        w_pair = jnp.concatenate([head_weight, w_p], 1)
        w_all = jnp.concatenate([w_pair, swap(w_pair, "dl")], 1)
        for s in range(n):
            if n > 4:
                src = (dh - s) % n
                h_s, t_s = gathered_h[src], gathered_t[src]
                values = whole_rows(h_s, t, nt)
            elif s == 0:
                h_s, t_s = hidden_states, target_ids
                values = whole_rows(h_s, t, nt)
            else:
                h_s, t_s = moved[s - 1], moved_t[s - 1]
                values = whole_rows(h_s, t, nt)
            stats.append(block_stats(values, t_s, w_all))
    stats = jnp.stack(stats)
    stats = jnp.take(stats, (dh - jnp.arange(n)) % n, axis=0)
    rq = rb // nt
    stats = stats.reshape(n, 4, nt, rq).transpose(0, 2, 1, 3).reshape(n * nt, 4, rq)
    got = lax.all_to_all(stats, ("dh", "t"), 0, 0, tiled=True)
    tops, totals, spreads, pickeds = got[:, 0], got[:, 1], got[:, 2], got[:, 3]
    row_top = jnp.max(tops, axis=0)
    scale = jnp.exp(tops - row_top[None, :])
    row_total = jnp.sum(totals * scale, axis=0)
    row_spread = jnp.sum(scale * (spreads + totals * (tops - row_top[None, :])), axis=0)
    row_picked = jnp.sum(pickeds, axis=0)

    logsum = jnp.log(row_total)
    live = lax.dynamic_slice_in_dim(loss_mask, t * rq, rq).astype(jnp.float32)
    token_logprob = (row_picked - row_top - logsum) * live
    token_entropy = (logsum - row_spread / row_total) * live

    seqs = slot_order.shape[0]
    ends = jnp.cumsum(seq_lengths)
    position = b * rb + t * rq + jnp.arange(rq, dtype=jnp.int32)
    segment = jnp.sum((position[:, None] >= ends[None, :]).astype(jnp.int32), axis=1)
    member = segment[:, None] == slot_order[None, :]
    rowwise = jnp.stack([token_logprob, token_entropy, live])
    k = seqs // nd
    parts = jnp.sum(jnp.where(member[None], rowwise[:, :, None], 0.0), axis=1)
    parts = parts.reshape(3, nd, k).transpose(1, 0, 2)
    parts = jnp.broadcast_to(parts[:, None], (nd, nt, 3, k)).reshape(nd * nt, 3, k)
    sums = jnp.sum(lax.all_to_all(parts, ALL, 0, 0, tiled=True), axis=0)
    floor = jnp.maximum(sums[2], 1.0)
    return (token_logprob, token_entropy, sums[0] / floor, sums[1] / floor)


def solution(mesh):
    nd, nt = mesh.devices.shape
    grid = Mesh(mesh.devices.reshape(nd // 4, 2, 2, nt), ALL)
    placed = (P(ROWS, "t"), P(), P(None, ("t",) + ROWS), P(ROWS), P(ROWS), P(), P())
    return jax.shard_map(
        per_device,
        mesh=grid,
        in_specs=placed,
        out_specs=(P(ALL), P(ALL), P(ROWS), P(ROWS)),
        check_vma=False,
    )
```

```python
import jax
import jax.numpy as jnp
import numpy as np
from jax import lax
from jax.sharding import Mesh
from jax.sharding import PartitionSpec as P

EPS = 1e-05
ROWS = ("dh", "p", "dl")
ALL = ("dh", "p", "dl", "t")


def swap(x, name):
    return lax.ppermute(x, name, [(0, 1), (1, 0)])


def whole_rows(x, t, nt, other=None):
    if nt == 2:
        if other is None:
            other = swap(x, "t")
        return jnp.where(t == 0, jnp.concatenate([x, other], 1), jnp.concatenate([other, x], 1))
    return lax.all_gather(x, "t", axis=1, tiled=True)


def shifted(x, s, n, dh):
    if s == 0:
        return x
    if n <= 4:
        return lax.ppermute(x, "dh", [(i, (i + s) % n) for i in range(n)])
    return None


def per_device(hidden_states, norm_gain, head_weight, target_ids, loss_mask, seq_lengths, slot_order):
    rb, dt = hidden_states.shape
    nt = lax.axis_size("t")
    n = lax.axis_size("dh")
    nd = n * 4
    d = dt * nt
    cb = head_weight.shape[1]
    t = lax.axis_index("t")
    dh = lax.axis_index("dh")
    p = lax.axis_index("p")
    dl = lax.axis_index("dl")
    b = (dh * 2 + p) * 2 + dl

    w_p = swap(head_weight, "p")
    block_of = jnp.stack([b, (dh * 2 + 1 - p) * 2 + dl, (dh * 2 + p) * 2 + 1 - dl, (dh * 2 + 1 - p) * 2 + 1 - dl])
    column = ((t * nd + block_of)[:, None] * cb + jnp.arange(cb, dtype=jnp.int32)[None, :]).reshape(-1)

    gain = norm_gain.astype(jnp.float32)
    if n > 4:
        gathered_h = lax.all_gather(hidden_states, "dh", axis=0, tiled=False)
        gathered_t = lax.all_gather(target_ids, "dh", axis=0, tiled=False)

    else:
        fast = nt == 2 and (2 * rb) % dt == 0
        if not fast:
            moved = [shifted(hidden_states, s, n, dh) for s in range(1, n)]
            moved_t = [shifted(target_ids, s, n, dh) for s in range(1, n)]
            w_p, moved, moved_t = lax.optimization_barrier((w_p, moved, moved_t))

    def normalize(values):
        values = values.astype(jnp.float32)
        square = jnp.mean(values * values, axis=1, keepdims=True)
        return (values * lax.rsqrt(square + EPS) * gain[None, :]).astype(jnp.bfloat16)

    def block_stats(values, t_s, w_all, col=None):
        col = column if col is None else col
        logits = jnp.dot(normalize(values), w_all, preferred_element_type=jnp.float32)
        top = jnp.max(logits, axis=1)
        shift = logits - top[:, None]
        expo = jnp.exp(shift)
        total = jnp.sum(expo, axis=1)
        spread = jnp.sum(expo * shift, axis=1)
        picked = jnp.sum(jnp.where(col[None, :] == t_s[:, None], logits, 0.0), axis=1)
        return jnp.stack([top, total, spread, picked])

    def combine(pieces):
        got = jnp.stack(pieces)
        tops, totals, spreads, pickeds = got[:, 0], got[:, 1], got[:, 2], got[:, 3]
        top = jnp.max(tops, axis=0)
        scale = jnp.exp(tops - top[None, :])
        total = jnp.sum(totals * scale, axis=0)
        spread = jnp.sum(scale * (spreads + totals * (tops - top[None, :])), axis=0)
        return jnp.stack([top, total, spread, jnp.sum(pickeds, axis=0)])

    def joined(x, other):
        return jnp.where(t == 0, jnp.concatenate([x, other], 1), jnp.concatenate([other, x], 1))

    stats = []
    if n <= 4 and fast:
        extra = (2 * rb) // dt
        code = jnp.concatenate([target_ids // 128, target_ids % 128]).astype(jnp.bfloat16).reshape(extra, dt)
        carried = jnp.concatenate([hidden_states, code], 0)
        near = [s for s in sorted({1, n - 1}) if 1 <= s < n]
        far = [s for s in range(1, n) if s not in near]
        cols = [column[i * cb:(i + 1) * cb] for i in range(4)]

        def unpack(block):
            parts = block[rb:].reshape(2, rb).astype(jnp.int32)
            return block[:rb], parts[0] * 128 + parts[1]

        own_other, w_c, got = lax.optimization_barrier(
            (swap(hidden_states, "t"), swap(head_weight, "dl"), [shifted(carried, s, n, dh) for s in near]))
        rows = {0: (hidden_states, target_ids)}
        for s, block in zip(near, got):
            rows[s] = unpack(block)
        values = {0: joined(hidden_states, own_other)}
        w_own = jnp.concatenate([head_weight, w_c], 1)
        c_own = jnp.concatenate([cols[0], cols[2]])
        held = ((w_own, c_own), (w_p, cols[1]))
        first = [block_stats(values[0], target_ids, w, c) for w, c in held]
        pending_far = [shifted(carried, s, n, dh) for s in far]
        early = {}
        if near:
            first, lead_other, held_rows = lax.optimization_barrier(
                (first, swap(rows[near[0]][0], "t"), [rows[s][0] for s in near[1:]]))
            for s, block in zip(near[1:], held_rows):
                rows[s] = (block, rows[s][1])
            values[near[0]] = joined(rows[near[0]][0], lead_other)
            lead_stats = [block_stats(values[near[0]], rows[near[0]][1], w, c) for w, c in held]
            lead_stats, rest, got = lax.optimization_barrier(
                (lead_stats, [swap(rows[s][0], "t") for s in near[1:]], pending_far))
            early[near[0]] = lead_stats
            for s, other in zip(near[1:], rest):
                values[s] = joined(rows[s][0], other)
        else:
            first, got = lax.optimization_barrier((first, pending_far))
        early[0] = first
        for s, block in zip(far, got):
            rows[s] = unpack(block)
        later = {s: [block_stats(values[s], rows[s][1], w, c) for w, c in held] for s in near[1:]}
        later, w_d, others = lax.optimization_barrier(
            (later, swap(w_p, "dl"), [swap(rows[s][0], "t") for s in far]))
        early.update(later)
        for s, other in zip(far, others):
            values[s] = joined(rows[s][0], other)
        pieces = held + ((w_d, cols[3]),)
        for s in range(n):
            if s in early:
                parts = early[s] + [block_stats(values[s], rows[s][1], w_d, cols[3])]
            else:
                parts = [block_stats(values[s], rows[s][1], w, c) for w, c in pieces]
            stats.append(combine(parts))
    else:
        w_pair = jnp.concatenate([head_weight, w_p], 1)
        w_all = jnp.concatenate([w_pair, swap(w_pair, "dl")], 1)
        for s in range(n):
            if n > 4:
                src = (dh - s) % n
                h_s, t_s = gathered_h[src], gathered_t[src]
                values = whole_rows(h_s, t, nt)
            elif s == 0:
                h_s, t_s = hidden_states, target_ids
                values = whole_rows(h_s, t, nt)
            else:
                h_s, t_s = moved[s - 1], moved_t[s - 1]
                values = whole_rows(h_s, t, nt)
            stats.append(block_stats(values, t_s, w_all))
    stats = jnp.stack(stats)
    stats = jnp.take(stats, (dh - jnp.arange(n)) % n, axis=0)
    rq = rb // nt
    stats = stats.reshape(n, 4, nt, rq).transpose(0, 2, 1, 3).reshape(n * nt, 4, rq)
    got = lax.all_to_all(stats, ("dh", "t"), 0, 0, tiled=True)
    tops, totals, spreads, pickeds = got[:, 0], got[:, 1], got[:, 2], got[:, 3]
    row_top = jnp.max(tops, axis=0)
    scale = jnp.exp(tops - row_top[None, :])
    row_total = jnp.sum(totals * scale, axis=0)
    row_spread = jnp.sum(scale * (spreads + totals * (tops - row_top[None, :])), axis=0)
    row_picked = jnp.sum(pickeds, axis=0)

    logsum = jnp.log(row_total)
    live = lax.dynamic_slice_in_dim(loss_mask, t * rq, rq).astype(jnp.float32)
    token_logprob = (row_picked - row_top - logsum) * live
    token_entropy = (logsum - row_spread / row_total) * live

    seqs = slot_order.shape[0]
    ends = jnp.cumsum(seq_lengths)
    position = b * rb + t * rq + jnp.arange(rq, dtype=jnp.int32)
    segment = jnp.sum((position[:, None] >= ends[None, :]).astype(jnp.int32), axis=1)
    member = segment[:, None] == slot_order[None, :]
    rowwise = jnp.stack([token_logprob, token_entropy, live])
    k = seqs // nd
    parts = jnp.sum(jnp.where(member[None], rowwise[:, :, None], 0.0), axis=1)
    parts = parts.reshape(3, nd, k).transpose(1, 0, 2)
    parts = jnp.broadcast_to(parts[:, None], (nd, nt, 3, k)).reshape(nd * nt, 3, k)
    sums = jnp.sum(lax.all_to_all(parts, ALL, 0, 0, tiled=True), axis=0)
    floor = jnp.maximum(sums[2], 1.0)
    return (token_logprob, token_entropy, sums[0] / floor, sums[1] / floor)


def solution(mesh):
    nd, nt = mesh.devices.shape
    grid = Mesh(mesh.devices.reshape(nd // 4, 2, 2, nt), ALL)
    placed = (P(ROWS, "t"), P(), P(None, ("t",) + ROWS), P(ROWS), P(ROWS), P(), P())
    return jax.shard_map(
        per_device,
        mesh=grid,
        in_specs=placed,
        out_specs=(P(ALL), P(ALL), P(ROWS), P(ROWS)),
        check_vma=False,
    )
```

```python
import jax
import jax.numpy as jnp
import numpy as np
from jax import lax
from jax.sharding import Mesh
from jax.sharding import PartitionSpec as P

EPS = 1e-05
ROWS = ("dh", "p", "dl")
ALL = ("dh", "p", "dl", "t")


def swap(x, name):
    return lax.ppermute(x, name, [(0, 1), (1, 0)])


def whole_rows(x, t, nt, other=None):
    if nt == 2:
        if other is None:
            other = swap(x, "t")
        return jnp.where(t == 0, jnp.concatenate([x, other], 1), jnp.concatenate([other, x], 1))
    return lax.all_gather(x, "t", axis=1, tiled=True)


def shifted(x, s, n, dh):
    if s == 0:
        return x
    if n <= 4:
        return lax.ppermute(x, "dh", [(i, (i + s) % n) for i in range(n)])
    return None


def per_device(hidden_states, norm_gain, head_weight, target_ids, loss_mask, seq_lengths, slot_order):
    rb, dt = hidden_states.shape
    nt = lax.axis_size("t")
    n = lax.axis_size("dh")
    nd = n * 4
    d = dt * nt
    cb = head_weight.shape[1]
    t = lax.axis_index("t")
    dh = lax.axis_index("dh")
    p = lax.axis_index("p")
    dl = lax.axis_index("dl")
    b = (dh * 2 + p) * 2 + dl

    w_p = swap(head_weight, "p")
    block_of = jnp.stack([b, (dh * 2 + 1 - p) * 2 + dl, (dh * 2 + p) * 2 + 1 - dl, (dh * 2 + 1 - p) * 2 + 1 - dl])
    column = ((t * nd + block_of)[:, None] * cb + jnp.arange(cb, dtype=jnp.int32)[None, :]).reshape(-1)

    gain = norm_gain.astype(jnp.float32)
    if n > 4:
        gathered_h = lax.all_gather(hidden_states, "dh", axis=0, tiled=False)
        gathered_t = lax.all_gather(target_ids, "dh", axis=0, tiled=False)

    else:
        fast = nt == 2 and (2 * rb) % dt == 0
        if not fast:
            moved = [shifted(hidden_states, s, n, dh) for s in range(1, n)]
            moved_t = [shifted(target_ids, s, n, dh) for s in range(1, n)]
            w_p, moved, moved_t = lax.optimization_barrier((w_p, moved, moved_t))

    def normalize(values):
        values = values.astype(jnp.float32)
        square = jnp.mean(values * values, axis=1, keepdims=True)
        return (values * lax.rsqrt(square + EPS) * gain[None, :]).astype(jnp.bfloat16)

    def block_stats(values, t_s, w_all, col=None):
        col = column if col is None else col
        logits = jnp.dot(normalize(values), w_all, preferred_element_type=jnp.float32)
        top = jnp.max(logits, axis=1)
        shift = logits - top[:, None]
        expo = jnp.exp(shift)
        total = jnp.sum(expo, axis=1)
        spread = jnp.sum(expo * shift, axis=1)
        picked = jnp.sum(jnp.where(col[None, :] == t_s[:, None], logits, 0.0), axis=1)
        return jnp.stack([top, total, spread, picked])

    def combine(pieces):
        got = jnp.stack(pieces)
        tops, totals, spreads, pickeds = got[:, 0], got[:, 1], got[:, 2], got[:, 3]
        top = jnp.max(tops, axis=0)
        scale = jnp.exp(tops - top[None, :])
        total = jnp.sum(totals * scale, axis=0)
        spread = jnp.sum(scale * (spreads + totals * (tops - top[None, :])), axis=0)
        return jnp.stack([top, total, spread, jnp.sum(pickeds, axis=0)])

    def joined(x, other):
        return jnp.where(t == 0, jnp.concatenate([x, other], 1), jnp.concatenate([other, x], 1))

    stats = []
    if n <= 4 and fast:
        extra = (2 * rb) // dt
        code = jnp.concatenate([target_ids // 128, target_ids % 128]).astype(jnp.bfloat16).reshape(extra, dt)
        carried = jnp.concatenate([hidden_states, code], 0)
        near = [s for s in sorted({1, n - 1}) if 1 <= s < n]
        far = [s for s in range(1, n) if s not in near]
        cols = [column[i * cb:(i + 1) * cb] for i in range(4)]

        def unpack(block):
            parts = block[rb:].reshape(2, rb).astype(jnp.int32)
            return block[:rb], parts[0] * 128 + parts[1]

        own_other, w_c, got = lax.optimization_barrier(
            (swap(hidden_states, "t"), swap(head_weight, "dl"), [shifted(carried, s, n, dh) for s in near]))
        rows = {0: (hidden_states, target_ids)}
        for s, block in zip(near, got):
            rows[s] = unpack(block)
        values = {0: joined(hidden_states, own_other)}
        w_own = jnp.concatenate([head_weight, w_c], 1)
        c_own = jnp.concatenate([cols[0], cols[2]])
        held = ((w_own, c_own), (w_p, cols[1]))
        first = [block_stats(values[0], target_ids, w, c) for w, c in held]
        first, got, others, w_d = lax.optimization_barrier(
            (first, [shifted(carried, s, n, dh) for s in far], [swap(block, "t") for block in got], swap(w_p, "dl")))
        for s, block in zip(far, got):
            rows[s] = unpack(block)
        for s, other in zip(near, others):
            values[s] = joined(rows[s][0], other[:rb])
        pieces = held + ((w_d, cols[3]),)
        early = {s: [block_stats(values[s], rows[s][1], w, c) for w, c in pieces] for s in near[:1]}
        early, others = lax.optimization_barrier((early, [swap(block, "t") for block in got]))
        for s in near[1:]:
            early[s] = [block_stats(values[s], rows[s][1], w, c) for w, c in pieces]
        early[0] = first + [block_stats(values[0], target_ids, w_d, cols[3])]
        for s, other in zip(far, others):
            values[s] = joined(rows[s][0], other[:rb])
        for s in range(n):
            if s in early:
                parts = early[s]
            else:
                parts = [block_stats(values[s], rows[s][1], w, c) for w, c in pieces]
            stats.append(combine(parts))
    else:
        w_pair = jnp.concatenate([head_weight, w_p], 1)
        w_all = jnp.concatenate([w_pair, swap(w_pair, "dl")], 1)
        for s in range(n):
            if n > 4:
                src = (dh - s) % n
                h_s, t_s = gathered_h[src], gathered_t[src]
                values = whole_rows(h_s, t, nt)
            elif s == 0:
                h_s, t_s = hidden_states, target_ids
                values = whole_rows(h_s, t, nt)
            else:
                h_s, t_s = moved[s - 1], moved_t[s - 1]
                values = whole_rows(h_s, t, nt)
            stats.append(block_stats(values, t_s, w_all))
    stats = jnp.stack(stats)
    stats = jnp.take(stats, (dh - jnp.arange(n)) % n, axis=0)
    rq = rb // nt
    stats = stats.reshape(n, 4, nt, rq).transpose(0, 2, 1, 3).reshape(n * nt, 4, rq)
    got = lax.all_to_all(stats, ("dh", "t"), 0, 0, tiled=True)
    tops, totals, spreads, pickeds = got[:, 0], got[:, 1], got[:, 2], got[:, 3]
    row_top = jnp.max(tops, axis=0)
    scale = jnp.exp(tops - row_top[None, :])
    row_total = jnp.sum(totals * scale, axis=0)
    row_spread = jnp.sum(scale * (spreads + totals * (tops - row_top[None, :])), axis=0)
    row_picked = jnp.sum(pickeds, axis=0)

    logsum = jnp.log(row_total)
    live = lax.dynamic_slice_in_dim(loss_mask, t * rq, rq).astype(jnp.float32)
    token_logprob = (row_picked - row_top - logsum) * live
    token_entropy = (logsum - row_spread / row_total) * live

    seqs = slot_order.shape[0]
    ends = jnp.cumsum(seq_lengths)
    position = b * rb + t * rq + jnp.arange(rq, dtype=jnp.int32)
    segment = jnp.sum((position[:, None] >= ends[None, :]).astype(jnp.int32), axis=1)
    member = segment[:, None] == slot_order[None, :]
    rowwise = jnp.stack([token_logprob, token_entropy, live])
    k = seqs // nd
    parts = jnp.sum(jnp.where(member[None], rowwise[:, :, None], 0.0), axis=1)
    parts = parts.reshape(3, nd, k).transpose(1, 0, 2)
    parts = jnp.broadcast_to(parts[:, None], (nd, nt, 3, k)).reshape(nd * nt, 3, k)
    sums = jnp.sum(lax.all_to_all(parts, ALL, 0, 0, tiled=True), axis=0)
    floor = jnp.maximum(sums[2], 1.0)
    return (token_logprob, token_entropy, sums[0] / floor, sums[1] / floor)


def solution(mesh):
    nd, nt = mesh.devices.shape
    grid = Mesh(mesh.devices.reshape(nd // 4, 2, 2, nt), ALL)
    placed = (P(ROWS, "t"), P(), P(None, ("t",) + ROWS), P(ROWS), P(ROWS), P(), P())
    return jax.shard_map(
        per_device,
        mesh=grid,
        in_specs=placed,
        out_specs=(P(ALL), P(ALL), P(ROWS), P(ROWS)),
        check_vma=False,
    )
```

```python
import jax
import jax.numpy as jnp
import numpy as np
from jax import lax
from jax.sharding import Mesh
from jax.sharding import PartitionSpec as P

EPS = 1e-05
ROWS = ("dh", "p", "dl")
ALL = ("dh", "p", "dl", "t")


def swap(x, name):
    return lax.ppermute(x, name, [(0, 1), (1, 0)])


def whole_rows(x, t, nt, other=None):
    if nt == 2:
        if other is None:
            other = swap(x, "t")
        return jnp.where(t == 0, jnp.concatenate([x, other], 1), jnp.concatenate([other, x], 1))
    return lax.all_gather(x, "t", axis=1, tiled=True)


def shifted(x, s, n, dh):
    if s == 0:
        return x
    if n <= 4:
        return lax.ppermute(x, "dh", [(i, (i + s) % n) for i in range(n)])
    return None


def per_device(hidden_states, norm_gain, head_weight, target_ids, loss_mask, seq_lengths, slot_order):
    rb, dt = hidden_states.shape
    nt = lax.axis_size("t")
    n = lax.axis_size("dh")
    nd = n * 4
    d = dt * nt
    cb = head_weight.shape[1]
    t = lax.axis_index("t")
    dh = lax.axis_index("dh")
    p = lax.axis_index("p")
    dl = lax.axis_index("dl")
    b = (dh * 2 + p) * 2 + dl

    w_p = swap(head_weight, "p")
    block_of = jnp.stack([b, (dh * 2 + 1 - p) * 2 + dl, (dh * 2 + p) * 2 + 1 - dl, (dh * 2 + 1 - p) * 2 + 1 - dl])
    column = ((t * nd + block_of)[:, None] * cb + jnp.arange(cb, dtype=jnp.int32)[None, :]).reshape(-1)

    gain = norm_gain.astype(jnp.float32)
    if n > 4:
        gathered_h = lax.all_gather(hidden_states, "dh", axis=0, tiled=False)
        gathered_t = lax.all_gather(target_ids, "dh", axis=0, tiled=False)

    else:
        fast = nt == 2 and (2 * rb) % dt == 0
        if not fast:
            moved = [shifted(hidden_states, s, n, dh) for s in range(1, n)]
            moved_t = [shifted(target_ids, s, n, dh) for s in range(1, n)]
            w_p, moved, moved_t = lax.optimization_barrier((w_p, moved, moved_t))

    def normalize(values):
        values = values.astype(jnp.float32)
        square = jnp.mean(values * values, axis=1, keepdims=True)
        return (values * lax.rsqrt(square + EPS) * gain[None, :]).astype(jnp.bfloat16)

    def block_stats(values, t_s, w_all, col=None):
        col = column if col is None else col
        logits = jnp.dot(normalize(values), w_all, preferred_element_type=jnp.float32)
        top = jnp.max(logits, axis=1)
        shift = logits - top[:, None]
        expo = jnp.exp(shift)
        total = jnp.sum(expo, axis=1)
        spread = jnp.sum(expo * shift, axis=1)
        picked = jnp.sum(jnp.where(col[None, :] == t_s[:, None], logits, 0.0), axis=1)
        return jnp.stack([top, total, spread, picked])

    def combine(pieces):
        got = jnp.stack(pieces)
        tops, totals, spreads, pickeds = got[:, 0], got[:, 1], got[:, 2], got[:, 3]
        top = jnp.max(tops, axis=0)
        scale = jnp.exp(tops - top[None, :])
        total = jnp.sum(totals * scale, axis=0)
        spread = jnp.sum(scale * (spreads + totals * (tops - top[None, :])), axis=0)
        return jnp.stack([top, total, spread, jnp.sum(pickeds, axis=0)])

    def joined(x, other):
        return jnp.where(t == 0, jnp.concatenate([x, other], 1), jnp.concatenate([other, x], 1))

    stats = []
    if n <= 4 and fast:
        extra = (2 * rb) // dt
        code = jnp.concatenate([target_ids // 128, target_ids % 128]).astype(jnp.bfloat16).reshape(extra, dt)
        carried = jnp.concatenate([hidden_states, code], 0)
        near = [s for s in sorted({1, n - 1}) if 1 <= s < n]
        far = [s for s in range(1, n) if s not in near]
        cols = [column[i * cb:(i + 1) * cb] for i in range(4)]

        def unpack(block):
            parts = block[rb:].reshape(2, rb).astype(jnp.int32)
            return block[:rb], parts[0] * 128 + parts[1]

        own_other, w_c, got = lax.optimization_barrier(
            (swap(hidden_states, "t"), swap(head_weight, "dl"), [shifted(carried, s, n, dh) for s in near]))
        rows = {0: (hidden_states, target_ids)}
        for s, block in zip(near, got):
            rows[s] = unpack(block)
        values = {0: joined(hidden_states, own_other)}
        w_own = jnp.concatenate([head_weight, w_c], 1)
        c_own = jnp.concatenate([cols[0], cols[2]])
        held = ((w_own, c_own), (w_p, cols[1]))
        first = [block_stats(values[0], target_ids, w, c) for w, c in held]
        first, got, others = lax.optimization_barrier(
            (first, [shifted(carried, s, n, dh) for s in far], [swap(rows[s][0], "t") for s in near]))
        for s, block in zip(far, got):
            rows[s] = unpack(block)
        for s, other in zip(near, others):
            values[s] = joined(rows[s][0], other)
        early = {0: first}
        lead = near[0] if near else None
        lead_stats = [block_stats(values[lead], rows[lead][1], w, c) for w, c in held] if near else []
        lead_stats, w_d, others = lax.optimization_barrier(
            (lead_stats, swap(w_p, "dl"), [swap(rows[s][0], "t") for s in far]))
        if near:
            early[lead] = lead_stats
        for s, other in zip(far, others):
            values[s] = joined(rows[s][0], other)
        for s in near[1:]:
            early[s] = [block_stats(values[s], rows[s][1], w, c) for w, c in held]
        pieces = held + ((w_d, cols[3]),)
        blocks = []
        for s in range(n):
            if s in early:
                parts = early[s] + [block_stats(values[s], rows[s][1], w_d, cols[3])]
            else:
                parts = [block_stats(values[s], rows[s][1], w, c) for w, c in pieces]
            blocks.append(jnp.stack(parts))
        got = jnp.stack(blocks)
        tops, totals, spreads, pickeds = got[:, :, 0], got[:, :, 1], got[:, :, 2], got[:, :, 3]
        top = jnp.max(tops, axis=1)
        scale = jnp.exp(tops - top[:, None, :])
        total = jnp.sum(totals * scale, axis=1)
        spread = jnp.sum(scale * (spreads + totals * (tops - top[:, None, :])), axis=1)
        stats = jnp.stack([top, total, spread, jnp.sum(pickeds, axis=1)], axis=1)
    else:
        w_pair = jnp.concatenate([head_weight, w_p], 1)
        w_all = jnp.concatenate([w_pair, swap(w_pair, "dl")], 1)
        for s in range(n):
            if n > 4:
                src = (dh - s) % n
                h_s, t_s = gathered_h[src], gathered_t[src]
                values = whole_rows(h_s, t, nt)
            elif s == 0:
                h_s, t_s = hidden_states, target_ids
                values = whole_rows(h_s, t, nt)
            else:
                h_s, t_s = moved[s - 1], moved_t[s - 1]
                values = whole_rows(h_s, t, nt)
            stats.append(block_stats(values, t_s, w_all))
    stats = jnp.stack(stats) if isinstance(stats, list) else stats
    stats = jnp.take(stats, (dh - jnp.arange(n)) % n, axis=0)
    rq = rb // nt
    stats = stats.reshape(n, 4, nt, rq).transpose(0, 2, 1, 3).reshape(n * nt, 4, rq)
    got = lax.all_to_all(stats, ("dh", "t"), 0, 0, tiled=True)
    tops, totals, spreads, pickeds = got[:, 0], got[:, 1], got[:, 2], got[:, 3]
    row_top = jnp.max(tops, axis=0)
    scale = jnp.exp(tops - row_top[None, :])
    row_total = jnp.sum(totals * scale, axis=0)
    row_spread = jnp.sum(scale * (spreads + totals * (tops - row_top[None, :])), axis=0)
    row_picked = jnp.sum(pickeds, axis=0)

    logsum = jnp.log(row_total)
    live = lax.dynamic_slice_in_dim(loss_mask, t * rq, rq).astype(jnp.float32)
    token_logprob = (row_picked - row_top - logsum) * live
    token_entropy = (logsum - row_spread / row_total) * live

    seqs = slot_order.shape[0]
    ends = jnp.cumsum(seq_lengths)
    position = b * rb + t * rq + jnp.arange(rq, dtype=jnp.int32)
    segment = jnp.sum((position[:, None] >= ends[None, :]).astype(jnp.int32), axis=1)
    member = segment[:, None] == slot_order[None, :]
    rowwise = jnp.stack([token_logprob, token_entropy, live])
    k = seqs // nd
    parts = jnp.sum(jnp.where(member[None], rowwise[:, :, None], 0.0), axis=1)
    parts = parts.reshape(3, nd, k).transpose(1, 0, 2)
    parts = jnp.broadcast_to(parts[:, None], (nd, nt, 3, k)).reshape(nd * nt, 3, k)
    sums = jnp.sum(lax.all_to_all(parts, ALL, 0, 0, tiled=True), axis=0)
    floor = jnp.maximum(sums[2], 1.0)
    return (token_logprob, token_entropy, sums[0] / floor, sums[1] / floor)


def solution(mesh):
    nd, nt = mesh.devices.shape
    grid = Mesh(mesh.devices.reshape(nd // 4, 2, 2, nt), ALL)
    placed = (P(ROWS, "t"), P(), P(None, ("t",) + ROWS), P(ROWS), P(ROWS), P(), P())
    return jax.shard_map(
        per_device,
        mesh=grid,
        in_specs=placed,
        out_specs=(P(ALL), P(ALL), P(ROWS), P(ROWS)),
        check_vma=False,
    )
```

```python
import jax
import jax.numpy as jnp
import numpy as np
from jax import lax
from jax.sharding import Mesh
from jax.sharding import PartitionSpec as P

EPS = 1e-05
ROWS = ("dh", "p", "dl")
ALL = ("dh", "p", "dl", "t")


def swap(x, name):
    return lax.ppermute(x, name, [(0, 1), (1, 0)])


def whole_rows(x, t, nt, other=None):
    if nt == 2:
        if other is None:
            other = swap(x, "t")
        return jnp.where(t == 0, jnp.concatenate([x, other], 1), jnp.concatenate([other, x], 1))
    return lax.all_gather(x, "t", axis=1, tiled=True)


def shifted(x, s, n, dh):
    if s == 0:
        return x
    if n <= 4:
        return lax.ppermute(x, "dh", [(i, (i + s) % n) for i in range(n)])
    return None


def per_device(hidden_states, norm_gain, head_weight, target_ids, loss_mask, seq_lengths, slot_order):
    rb, dt = hidden_states.shape
    nt = lax.axis_size("t")
    n = lax.axis_size("dh")
    nd = n * 4
    d = dt * nt
    cb = head_weight.shape[1]
    t = lax.axis_index("t")
    dh = lax.axis_index("dh")
    p = lax.axis_index("p")
    dl = lax.axis_index("dl")
    b = (dh * 2 + p) * 2 + dl

    w_p = swap(head_weight, "p")
    block_of = jnp.stack([b, (dh * 2 + 1 - p) * 2 + dl, (dh * 2 + p) * 2 + 1 - dl, (dh * 2 + 1 - p) * 2 + 1 - dl])
    column = ((t * nd + block_of)[:, None] * cb + jnp.arange(cb, dtype=jnp.int32)[None, :]).reshape(-1)

    gain = norm_gain.astype(jnp.float32)
    if n > 4:
        gathered_h = lax.all_gather(hidden_states, "dh", axis=0, tiled=False)
        gathered_t = lax.all_gather(target_ids, "dh", axis=0, tiled=False)

    else:
        fast = nt == 2 and (2 * rb) % dt == 0
        if not fast:
            moved = [shifted(hidden_states, s, n, dh) for s in range(1, n)]
            moved_t = [shifted(target_ids, s, n, dh) for s in range(1, n)]
            w_p, moved, moved_t = lax.optimization_barrier((w_p, moved, moved_t))

    def normalize(values):
        values = values.astype(jnp.float32)
        square = jnp.mean(values * values, axis=1, keepdims=True)
        return (values * lax.rsqrt(square + EPS) * gain[None, :]).astype(jnp.bfloat16)

    def block_stats(values, t_s, w_all, col=None):
        col = column if col is None else col
        logits = jnp.dot(normalize(values), w_all, preferred_element_type=jnp.float32)
        top = jnp.max(logits, axis=1)
        shift = logits - top[:, None]
        expo = jnp.exp(shift)
        total = jnp.sum(expo, axis=1)
        spread = jnp.sum(expo * shift, axis=1)
        picked = jnp.sum(jnp.where(col[None, :] == t_s[:, None], logits, 0.0), axis=1)
        return jnp.stack([top, total, spread, picked])

    def combine(pieces):
        got = jnp.stack(pieces)
        tops, totals, spreads, pickeds = got[:, 0], got[:, 1], got[:, 2], got[:, 3]
        top = jnp.max(tops, axis=0)
        scale = jnp.exp(tops - top[None, :])
        total = jnp.sum(totals * scale, axis=0)
        spread = jnp.sum(scale * (spreads + totals * (tops - top[None, :])), axis=0)
        return jnp.stack([top, total, spread, jnp.sum(pickeds, axis=0)])

    def joined(x, other):
        return jnp.where(t == 0, jnp.concatenate([x, other], 1), jnp.concatenate([other, x], 1))

    stats = []
    if n <= 4 and fast:
        extra = (2 * rb) // dt
        code = jnp.concatenate([target_ids // 128, target_ids % 128]).astype(jnp.bfloat16).reshape(extra, dt)
        near = [s for s in sorted({1, n - 1}) if 1 <= s < n]
        far = [s for s in range(1, n) if s not in near]
        cols = [column[i * cb:(i + 1) * cb] for i in range(4)]

        def unpack(pair):
            block, coded = pair
            parts = coded.reshape(2, rb).astype(jnp.int32)
            return block, parts[0] * 128 + parts[1]

        def moved(s):
            return (shifted(hidden_states, s, n, dh), shifted(code, s, n, dh))

        own_other, w_c, got = lax.optimization_barrier(
            (swap(hidden_states, "t"), swap(head_weight, "dl"), [moved(s) for s in near]))
        rows = {0: (hidden_states, target_ids)}
        for s, block in zip(near, got):
            rows[s] = unpack(block)
        values = {0: joined(hidden_states, own_other)}
        w_own = jnp.concatenate([head_weight, w_c], 1)
        c_own = jnp.concatenate([cols[0], cols[2]])
        held = ((w_own, c_own), (w_p, cols[1]))
        first = [block_stats(values[0], target_ids, w, c) for w, c in held]
        first, got, others = lax.optimization_barrier(
            (first, [moved(s) for s in far], [swap(rows[s][0], "t") for s in near]))
        for s, block in zip(far, got):
            rows[s] = unpack(block)
        for s, other in zip(near, others):
            values[s] = joined(rows[s][0], other)
        early = {0: first}
        lead = near[0] if near else None
        lead_stats = [block_stats(values[lead], rows[lead][1], w, c) for w, c in held] if near else []
        lead_stats, w_d, others = lax.optimization_barrier(
            (lead_stats, swap(w_p, "dl"), [swap(rows[s][0], "t") for s in far]))
        if near:
            early[lead] = lead_stats
        for s, other in zip(far, others):
            values[s] = joined(rows[s][0], other)
        for s in near[1:]:
            early[s] = [block_stats(values[s], rows[s][1], w, c) for w, c in held]
        pieces = held + ((w_d, cols[3]),)
        for s in range(n):
            if s in early:
                parts = early[s] + [block_stats(values[s], rows[s][1], w_d, cols[3])]
            else:
                parts = [block_stats(values[s], rows[s][1], w, c) for w, c in pieces]
            stats.append(combine(parts))
    else:
        w_pair = jnp.concatenate([head_weight, w_p], 1)
        w_all = jnp.concatenate([w_pair, swap(w_pair, "dl")], 1)
        for s in range(n):
            if n > 4:
                src = (dh - s) % n
                h_s, t_s = gathered_h[src], gathered_t[src]
                values = whole_rows(h_s, t, nt)
            elif s == 0:
                h_s, t_s = hidden_states, target_ids
                values = whole_rows(h_s, t, nt)
            else:
                h_s, t_s = moved[s - 1], moved_t[s - 1]
                values = whole_rows(h_s, t, nt)
            stats.append(block_stats(values, t_s, w_all))
    stats = jnp.stack(stats)
    stats = jnp.take(stats, (dh - jnp.arange(n)) % n, axis=0)
    rq = rb // nt
    stats = stats.reshape(n, 4, nt, rq).transpose(0, 2, 1, 3).reshape(n * nt, 4, rq)
    got = lax.all_to_all(stats, ("dh", "t"), 0, 0, tiled=True)
    tops, totals, spreads, pickeds = got[:, 0], got[:, 1], got[:, 2], got[:, 3]
    row_top = jnp.max(tops, axis=0)
    scale = jnp.exp(tops - row_top[None, :])
    row_total = jnp.sum(totals * scale, axis=0)
    row_spread = jnp.sum(scale * (spreads + totals * (tops - row_top[None, :])), axis=0)
    row_picked = jnp.sum(pickeds, axis=0)

    logsum = jnp.log(row_total)
    live = lax.dynamic_slice_in_dim(loss_mask, t * rq, rq).astype(jnp.float32)
    token_logprob = (row_picked - row_top - logsum) * live
    token_entropy = (logsum - row_spread / row_total) * live

    seqs = slot_order.shape[0]
    ends = jnp.cumsum(seq_lengths)
    position = b * rb + t * rq + jnp.arange(rq, dtype=jnp.int32)
    segment = jnp.sum((position[:, None] >= ends[None, :]).astype(jnp.int32), axis=1)
    member = segment[:, None] == slot_order[None, :]
    rowwise = jnp.stack([token_logprob, token_entropy, live])
    k = seqs // nd
    parts = jnp.sum(jnp.where(member[None], rowwise[:, :, None], 0.0), axis=1)
    parts = parts.reshape(3, nd, k).transpose(1, 0, 2)
    parts = jnp.broadcast_to(parts[:, None], (nd, nt, 3, k)).reshape(nd * nt, 3, k)
    sums = jnp.sum(lax.all_to_all(parts, ALL, 0, 0, tiled=True), axis=0)
    floor = jnp.maximum(sums[2], 1.0)
    return (token_logprob, token_entropy, sums[0] / floor, sums[1] / floor)


def solution(mesh):
    nd, nt = mesh.devices.shape
    grid = Mesh(mesh.devices.reshape(nd // 4, 2, 2, nt), ALL)
    placed = (P(ROWS, "t"), P(), P(None, ("t",) + ROWS), P(ROWS), P(ROWS), P(), P())
    return jax.shard_map(
        per_device,
        mesh=grid,
        in_specs=placed,
        out_specs=(P(ALL), P(ALL), P(ROWS), P(ROWS)),
        check_vma=False,
    )
```

```python
import jax
import jax.numpy as jnp
import numpy as np
from jax import lax
from jax.sharding import Mesh
from jax.sharding import PartitionSpec as P

EPS = 1e-05
ROWS = ("dh", "p", "dl")
ALL = ("dh", "p", "dl", "t")


def swap(x, name):
    return lax.ppermute(x, name, [(0, 1), (1, 0)])


def whole_rows(x, t, nt, other=None):
    if nt == 2:
        if other is None:
            other = swap(x, "t")
        return jnp.where(t == 0, jnp.concatenate([x, other], 1), jnp.concatenate([other, x], 1))
    return lax.all_gather(x, "t", axis=1, tiled=True)


def shifted(x, s, n, dh):
    if s == 0:
        return x
    if n <= 4:
        return lax.ppermute(x, "dh", [(i, (i + s) % n) for i in range(n)])
    return None


def per_device(hidden_states, norm_gain, head_weight, target_ids, loss_mask, seq_lengths, slot_order):
    rb, dt = hidden_states.shape
    nt = lax.axis_size("t")
    n = lax.axis_size("dh")
    nd = n * 4
    d = dt * nt
    cb = head_weight.shape[1]
    t = lax.axis_index("t")
    dh = lax.axis_index("dh")
    p = lax.axis_index("p")
    dl = lax.axis_index("dl")
    b = (dh * 2 + p) * 2 + dl

    w_p = swap(head_weight, "p")
    block_of = jnp.stack([b, (dh * 2 + 1 - p) * 2 + dl, (dh * 2 + p) * 2 + 1 - dl, (dh * 2 + 1 - p) * 2 + 1 - dl])
    column = ((t * nd + block_of)[:, None] * cb + jnp.arange(cb, dtype=jnp.int32)[None, :]).reshape(-1)

    gain = norm_gain.astype(jnp.float32)
    if n > 4:
        gathered_h = lax.all_gather(hidden_states, "dh", axis=0, tiled=False)
        gathered_t = lax.all_gather(target_ids, "dh", axis=0, tiled=False)

    else:
        fast = nt == 2 and (2 * rb) % dt == 0
        if not fast:
            moved = [shifted(hidden_states, s, n, dh) for s in range(1, n)]
            moved_t = [shifted(target_ids, s, n, dh) for s in range(1, n)]
            w_p, moved, moved_t = lax.optimization_barrier((w_p, moved, moved_t))

    def normalize(values):
        values = values.astype(jnp.float32)
        square = jnp.mean(values * values, axis=1, keepdims=True)
        return (values * lax.rsqrt(square + EPS) * gain[None, :]).astype(jnp.bfloat16)

    def block_stats(values, t_s, w_all, col=None):
        return logit_stats(jnp.dot(normalize(values), w_all, preferred_element_type=jnp.float32), t_s, col)

    def logit_stats(logits, t_s, col=None):
        col = column if col is None else col
        top = jnp.max(logits, axis=1)
        shift = logits - top[:, None]
        expo = jnp.exp(shift)
        total = jnp.sum(expo, axis=1)
        spread = jnp.sum(expo * shift, axis=1)
        picked = jnp.sum(jnp.where(col[None, :] == t_s[:, None], logits, 0.0), axis=1)
        return jnp.stack([top, total, spread, picked])

    def ready(values):
        return lax.optimization_barrier(normalize(values))

    def ready_stats(normed, t_s, w_all, col):
        return logit_stats(jnp.dot(normed, w_all, preferred_element_type=jnp.float32), t_s, col)

    def combine(pieces):
        got = jnp.stack(pieces)
        tops, totals, spreads, pickeds = got[:, 0], got[:, 1], got[:, 2], got[:, 3]
        top = jnp.max(tops, axis=0)
        scale = jnp.exp(tops - top[None, :])
        total = jnp.sum(totals * scale, axis=0)
        spread = jnp.sum(scale * (spreads + totals * (tops - top[None, :])), axis=0)
        return jnp.stack([top, total, spread, jnp.sum(pickeds, axis=0)])

    def joined(x, other):
        return jnp.where(t == 0, jnp.concatenate([x, other], 1), jnp.concatenate([other, x], 1))

    stats = []
    if n <= 4 and fast:
        extra = (2 * rb) // dt
        code = jnp.concatenate([target_ids // 128, target_ids % 128]).astype(jnp.bfloat16).reshape(extra, dt)
        carried = jnp.concatenate([hidden_states, code], 0)
        near = [s for s in sorted({1, n - 1}) if 1 <= s < n]
        far = [s for s in range(1, n) if s not in near]
        cols = [column[i * cb:(i + 1) * cb] for i in range(4)]

        def unpack(block):
            parts = block[rb:].reshape(2, rb).astype(jnp.int32)
            return block[:rb], parts[0] * 128 + parts[1]

        own_other, w_c, got = lax.optimization_barrier(
            (swap(hidden_states, "t"), swap(head_weight, "dl"), [shifted(carried, s, n, dh) for s in near]))
        rows = {0: (hidden_states, target_ids)}
        for s, block in zip(near, got):
            rows[s] = unpack(block)
        values = {0: ready(joined(hidden_states, own_other))}
        w_own = jnp.concatenate([head_weight, w_c], 1)
        c_own = jnp.concatenate([cols[0], cols[2]])
        held = ((w_own, c_own), (w_p, cols[1]))
        first = [ready_stats(values[0], target_ids, w, c) for w, c in held]
        first, got, others = lax.optimization_barrier(
            (first, [shifted(carried, s, n, dh) for s in far], [swap(rows[s][0], "t") for s in near]))
        for s, block in zip(far, got):
            rows[s] = unpack(block)
        for s, other in zip(near, others):
            values[s] = ready(joined(rows[s][0], other))
        early = {0: first}
        lead = near[0] if near else None
        lead_stats = [ready_stats(values[lead], rows[lead][1], w, c) for w, c in held] if near else []
        lead_stats, w_d, others = lax.optimization_barrier(
            (lead_stats, swap(w_p, "dl"), [swap(rows[s][0], "t") for s in far]))
        if near:
            early[lead] = lead_stats
        for s, other in zip(far, others):
            values[s] = ready(joined(rows[s][0], other))
        for s in near[1:]:
            early[s] = [ready_stats(values[s], rows[s][1], w, c) for w, c in held]
        pieces = held + ((w_d, cols[3]),)
        for s in range(n):
            if s in early:
                parts = early[s] + [ready_stats(values[s], rows[s][1], w_d, cols[3])]
            else:
                parts = [ready_stats(values[s], rows[s][1], w, c) for w, c in pieces]
            stats.append(combine(parts))
    else:
        w_pair = jnp.concatenate([head_weight, w_p], 1)
        w_all = jnp.concatenate([w_pair, swap(w_pair, "dl")], 1)
        for s in range(n):
            if n > 4:
                src = (dh - s) % n
                h_s, t_s = gathered_h[src], gathered_t[src]
                values = whole_rows(h_s, t, nt)
            elif s == 0:
                h_s, t_s = hidden_states, target_ids
                values = whole_rows(h_s, t, nt)
            else:
                h_s, t_s = moved[s - 1], moved_t[s - 1]
                values = whole_rows(h_s, t, nt)
            stats.append(block_stats(values, t_s, w_all))
    stats = jnp.stack(stats)
    stats = jnp.take(stats, (dh - jnp.arange(n)) % n, axis=0)
    rq = rb // nt
    stats = stats.reshape(n, 4, nt, rq).transpose(0, 2, 1, 3).reshape(n * nt, 4, rq)
    got = lax.all_to_all(stats, ("dh", "t"), 0, 0, tiled=True)
    tops, totals, spreads, pickeds = got[:, 0], got[:, 1], got[:, 2], got[:, 3]
    row_top = jnp.max(tops, axis=0)
    scale = jnp.exp(tops - row_top[None, :])
    row_total = jnp.sum(totals * scale, axis=0)
    row_spread = jnp.sum(scale * (spreads + totals * (tops - row_top[None, :])), axis=0)
    row_picked = jnp.sum(pickeds, axis=0)

    logsum = jnp.log(row_total)
    live = lax.dynamic_slice_in_dim(loss_mask, t * rq, rq).astype(jnp.float32)
    token_logprob = (row_picked - row_top - logsum) * live
    token_entropy = (logsum - row_spread / row_total) * live

    seqs = slot_order.shape[0]
    ends = jnp.cumsum(seq_lengths)
    position = b * rb + t * rq + jnp.arange(rq, dtype=jnp.int32)
    segment = jnp.sum((position[:, None] >= ends[None, :]).astype(jnp.int32), axis=1)
    member = segment[:, None] == slot_order[None, :]
    rowwise = jnp.stack([token_logprob, token_entropy, live])
    k = seqs // nd
    parts = jnp.sum(jnp.where(member[None], rowwise[:, :, None], 0.0), axis=1)
    parts = parts.reshape(3, nd, k).transpose(1, 0, 2)
    parts = jnp.broadcast_to(parts[:, None], (nd, nt, 3, k)).reshape(nd * nt, 3, k)
    sums = jnp.sum(lax.all_to_all(parts, ALL, 0, 0, tiled=True), axis=0)
    floor = jnp.maximum(sums[2], 1.0)
    return (token_logprob, token_entropy, sums[0] / floor, sums[1] / floor)


def solution(mesh):
    nd, nt = mesh.devices.shape
    grid = Mesh(mesh.devices.reshape(nd // 4, 2, 2, nt), ALL)
    placed = (P(ROWS, "t"), P(), P(None, ("t",) + ROWS), P(ROWS), P(ROWS), P(), P())
    return jax.shard_map(
        per_device,
        mesh=grid,
        in_specs=placed,
        out_specs=(P(ALL), P(ALL), P(ROWS), P(ROWS)),
        check_vma=False,
    )
```
